128 devices in a mesh: gx: 16 (over x, z_lo, core), gy: 8 (over z_hi, y).
Axes of the slice: x: 4, y: 4, z: 4 (z_hi: 2, z_lo: 2; z = z_hi * 2 + z_lo), core: 2. Of those that a mesh axis runs over, the one named last changes fastest.
Arguments:
- points_rhs: float32 [16, 2097152], P(None, ('gx', 'gy')), may hold values from -6 to 6
- morton_order: int32 [2097152], P(('gx', 'gy')), may hold values from 0 to 16383, as said below
- band_offsets: int32 [8192], P(('gx', 'gy')), may hold values from -16 to 16, as said below
- leaf_basis: bfloat16 [8192, 32, 256], P(('gx', 'gy')), may hold values from -0.375 to 0.375
- band_blocks: bfloat16 [8192, 2, 256, 256], P(('gx', 'gy')), may hold values from -0.375 to 0.375
- translations: float32 [128, 7, 8, 2, 32, 32], P(('gx', 'gy'))
- out_basis: bfloat16 [8192, 32, 256], P(('gx', 'gy')), may hold values from -1 to 1
Outputs:
- transformed: float32 [16, 2097152], P(None, ('gx', 'gy'))
The draws below stay inside these ranges and needn't reach their ends.
Inputs may be any that keep to these rules, and one draw needn't show every extreme that they name: `morton_order`: for every node k, entries 16384 * k to 16384 * (k + 1) - 1 hold each of 0 to 16383 exactly once. `band_offsets`: never zero; the first leaf of every node has offset -16 and the last leaf of every node has offset 16.
All inputs are finite; a program needn't handle non-finite values.
Results may differ from the reference program's by a relative error of at most 0.0033.
Values may be sent and summed in bfloat16 or wider, within the bound.
No kernel may reach another device: no remote copies, remote signals or barrier semaphores. Data moves between devices by JAX's collectives and lax.ppermute only.
A program may use at most 128 MiB of HBM per device.

```python
import math
import jax
import jax.numpy as jnp
from jax import lax

R = 32
LEAF = 256
NRHS = 16
GROUPS = 8
LEAVES_DEV = 64
HW = 16
LEVELS = 7
NODES = 128
PTS_DEV = 16384
LEAVES = 8192
NPTS = 2097152


def shuffle_node(node_key):
    return jax.random.permutation(node_key, PTS_DEV)


def draw_morton_order(key, part):
    node_keys = jax.random.split(key, NODES)
    shuffled = jax.vmap(shuffle_node)(node_keys).astype(jnp.int32)
    return shuffled.reshape(NODES * PTS_DEV).astype(jnp.int32)


def draw_band_offsets(key, part):
    key_size, key_sign = jax.random.split(jax.random.fold_in(key, 7), 2)
    magnitude = jax.random.randint(key_size, (LEAVES,), 1, HW + 1).astype(jnp.int32)
    sign = (jax.random.randint(key_sign, (LEAVES,), 0, 2) * 2 - 1).astype(jnp.int32)
    drawn = (magnitude * sign).astype(jnp.int32)
    position = jnp.arange(LEAVES, dtype=jnp.int32) % LEAVES_DEV
    lowest = jnp.full((LEAVES,), -HW, dtype=jnp.int32)
    highest = jnp.full((LEAVES,), HW, dtype=jnp.int32)
    drawn = jnp.where(position == 0, lowest, drawn)
    drawn = jnp.where(position == LEAVES_DEV - 1, highest, drawn)
    return drawn.astype(jnp.int32)


def draw_translations(key, part):
    key_noise, key_diag = jax.random.split(key, 2)
    full_shape = (NODES, LEVELS, GROUPS, 2, R, R)
    jitter = jax.random.normal(key_noise, full_shape, jnp.float32)
    diagonal = jax.random.uniform(key_diag, (NODES, LEVELS, GROUPS, 1, R, 1), jnp.float32, 0.55, 0.85)
    identity = jnp.eye(R, dtype=jnp.float32)
    self_mask = (jnp.arange(2) == 0).astype(jnp.float32).reshape(1, 1, 1, 2, 1, 1)
    spread = (0.15 * self_mask + 0.7 * (1.0 - self_mask)) / math.sqrt(R)
    return (jitter * spread + self_mask * diagonal * identity).astype(jnp.float32)


def block_scale(stream_key, dims, pieces, smallest, top_value):
    level = 1.0
    for dim, blocks in pieces:
        steps = jax.random.uniform(jax.random.fold_in(jax.random.fold_in(stream_key, 6), dim), (blocks,), jnp.float32, smallest / len(pieces), top_value / len(pieces))
        level = level * jnp.repeat(jnp.exp(steps), dims[dim] // blocks).reshape((-1,) + (1,) * (len(dims) - 1 - dim))
    return level


def scatter_about(stream_key, shape, scale, limit, shards=(), held_as=jnp.bfloat16):
    values = jax.random.normal(stream_key, shape, jnp.float32) * scale
    if len(shards) > 0:
        values = block_scale(stream_key, shape, shards, -0.22, 0.18) * values
    return jnp.clip(values, min=-limit, max=limit).astype(held_as)


def setup_inputs(seed: int = 0) -> dict:
    key_list = jax.random.split(jax.random.key(seed), 8)
    return {
        "points_rhs": scatter_about(key_list[0], (NRHS, NPTS), 1.0, 6.0, ((1, 128),), jnp.float32),
        "morton_order": draw_morton_order(jax.random.fold_in(key_list[7], 71), 0),
        "band_offsets": draw_band_offsets(jax.random.fold_in(key_list[7], 71), 0),
        "leaf_basis": scatter_about(key_list[3], (LEAVES, R, LEAF), LEAF ** -0.5, 0.375, ((0, 128),)),
        "band_blocks": scatter_about(key_list[4], (LEAVES, 2, LEAF, LEAF), LEAF ** -0.5, 0.375, ((0, 128),)),
        "translations": draw_translations(jax.random.fold_in(key_list[7], 71), 0),
        "out_basis": scatter_about(key_list[6], (LEAVES, R, LEAF), R ** -0.5, 1.0, ((0, 128),)),
    }


def node_near(node_pair):
    bands, own_block, partner_block = node_pair
    bands_f = bands.astype(jnp.float32)
    own_term = jnp.einsum('lpq,slq->slp', bands_f[:, 0], own_block.astype(jnp.float32), precision=lax.Precision.HIGHEST)
    partner_term = jnp.einsum('lpq,slq->slp', bands_f[:, 1], partner_block.astype(jnp.float32), precision=lax.Precision.HIGHEST)
    return own_term + partner_term


def reference(points_rhs, morton_order, band_offsets, leaf_basis, band_blocks, translations, out_basis):
    node_start = (jnp.arange(NODES, dtype=jnp.int32) * PTS_DEV)[:, None]
    global_order = (morton_order.astype(jnp.int32).reshape(NODES, PTS_DEV) + node_start).reshape(NPTS)
    ordered = points_rhs[:, global_order].astype(jnp.bfloat16)
    leaves = ordered.reshape(NRHS, LEAVES, LEAF).astype(jnp.float32)
    coeffs = jnp.einsum('lrp,slp->lrs', leaf_basis.astype(jnp.float32), leaves, precision=lax.Precision.HIGHEST)
    width = LEAVES_DEV * NRHS
    group_cols = width // GROUPS
    coeffs = coeffs.reshape(NODES, LEAVES_DEV, R, NRHS).transpose(0, 2, 1, 3).reshape(NODES, R, GROUPS, group_cols)
    for level in range(LEVELS):
        stride = 2 ** level
        paired = coeffs.reshape(NODES // (2 * stride), 2, stride, R, GROUPS, group_cols)
        partner = paired[:, ::-1].reshape(NODES, R, GROUPS, group_cols)
        coeffs = jnp.einsum('dgab,dbgm->dagm', translations[:, level, :, 0], coeffs, precision=lax.Precision.HIGHEST) + jnp.einsum('dgab,dbgm->dagm', translations[:, level, :, 1], partner, precision=lax.Precision.HIGHEST)
    coeff_bf = coeffs.astype(jnp.bfloat16).reshape(NODES, R, LEAVES_DEV, NRHS).transpose(0, 2, 1, 3).reshape(LEAVES, R, NRHS)
    far_term = jnp.einsum('lrp,lrs->slp', out_basis.astype(jnp.float32), coeff_bf.astype(jnp.float32), precision=lax.Precision.HIGHEST).reshape(NRHS, NPTS)
    padded = jnp.pad(ordered, ((0, 0), (HW * LEAF, HW * LEAF))).reshape(NRHS, LEAVES + 2 * HW, LEAF)
    block_index = jnp.arange(LEAVES, dtype=jnp.int32) + HW + band_offsets.astype(jnp.int32)
    picked = jnp.take(padded, block_index, axis=1)
    picked_nodes = picked.reshape(NRHS, NODES, LEAVES_DEV, LEAF).transpose(1, 0, 2, 3)
    own_nodes = ordered.reshape(NRHS, NODES, LEAVES_DEV, LEAF).transpose(1, 0, 2, 3)
    blocks_nodes = band_blocks.reshape(NODES, LEAVES_DEV, 2, LEAF, LEAF)
    near_nodes = lax.map(node_near, (blocks_nodes, own_nodes, picked_nodes))
    near_term = near_nodes.transpose(1, 0, 2, 3).reshape(NRHS, NPTS)
    return far_term + near_term
```

```python
import jax
import jax.numpy as jnp
from jax import lax
from jax.experimental import pallas as pl
from jax.experimental.pallas import tpu as pltpu
from jax.sharding import PartitionSpec as P

HW = 16


ROWS = 32


def gather_kernel(idx_ref, x_ref, o_ref):
    def body(i, carry):
        base = pl.multiple_of(i * ROWS, ROWS)
        for g in range(ROWS // 8):
            rows = [x_ref[pl.ds(idx_ref[base + g * 8 + u], 1), :] for u in range(8)]
            o_ref[pl.ds(pl.multiple_of(base + g * 8, 8), 8), :] = jnp.concatenate(rows, axis=0)
        return carry

    lax.fori_loop(0, o_ref.shape[0] // ROWS, body, 0)


def row_gather(rows, index):
    count, width = rows.shape
    return pl.pallas_call(
        gather_kernel,
        out_shape=jax.ShapeDtypeStruct((count, width), rows.dtype),
        in_specs=[pl.BlockSpec(memory_space=pltpu.SMEM), pl.BlockSpec(memory_space=pltpu.VMEM)],
        out_specs=pl.BlockSpec(memory_space=pltpu.VMEM),
        compiler_params=pltpu.CompilerParams(vmem_limit_bytes=40 * 1024 * 1024),
        cost_estimate=pl.CostEstimate(flops=0, transcendentals=0, bytes_accessed=2 * count * width * 4),
    )(index, rows)


def from_partner(x, axis, distance):
    return lax.ppermute(x, axis, [(i, i ^ 1 << distance) for i in range(lax.axis_size(axis))])


def extended(x, sides, width):
    for axis, dim in sides:
        count, length = (lax.axis_size(axis), x.shape[dim])
        up = [(i, (i + 1) % count) for i in range(count - 1)]
        down = [(j, i) for i, j in up]
        last = lax.slice_in_dim(x, length - width, length, axis=dim)
        initial = lax.slice_in_dim(x, 0, width, axis=dim)
        before = lax.ppermute(last, axis, up)
        after = lax.ppermute(initial, axis, down)
        x = jnp.concatenate([before, x, after], axis=dim)
    return x


def translate(level_weights, own_coeffs, other_coeffs):
    first = jnp.einsum(
        "gab,bgm->agm",
        level_weights[:, 0],
        own_coeffs,
        precision=lax.Precision.HIGHEST,
        preferred_element_type=jnp.float32,
    )
    second = jnp.einsum(
        "gab,bgm->agm",
        level_weights[:, 1],
        other_coeffs,
        precision=lax.Precision.HIGHEST,
        preferred_element_type=jnp.float32,
    )
    return first + second


def local(points_rhs, morton_order, band_offsets, leaf_basis, band_blocks, translations, out_basis):
    rhs_count, point_count = points_rhs.shape
    leaf_count, rank_size, leaf_size = leaf_basis.shape
    group_total = translations.shape[2]
    total_cols = leaf_count * rhs_count
    group_width = total_cols // group_total
    ordered = row_gather(points_rhs.T, morton_order).T.astype(jnp.bfloat16)
    leaves = ordered.reshape(rhs_count, leaf_count, leaf_size)
    coeffs = jnp.einsum(
        "lrp,slp->rls", leaf_basis, leaves, preferred_element_type=jnp.float32
    ).reshape(rank_size, total_cols)
    weights = translations[0]
    low_bits = lax.axis_size("gy").bit_length() - 1
    high_bits = lax.axis_size("gx").bit_length() - 1
    coeffs = coeffs.reshape(rank_size, group_total, group_width)
    for level_bit in range(low_bits):
        partner = from_partner(coeffs, "gy", level_bit)
        coeffs = translate(weights[level_bit], coeffs, partner)
    for level_bit in range(high_bits):
        partner = from_partner(coeffs, "gx", level_bit)
        coeffs = translate(weights[low_bits + level_bit], coeffs, partner)
    coeffs = coeffs.reshape(rank_size, total_cols)
    coeff_bf = coeffs.astype(jnp.bfloat16).reshape(rank_size, leaf_count, rhs_count)
    far_term = jnp.einsum("lrp,rls->slp", out_basis, coeff_bf, preferred_element_type=jnp.float32)
    padded = extended(ordered, ((("gx", "gy"), 1),), HW * leaf_size)
    blocks_all = padded.reshape(rhs_count, leaf_count + 2 * HW, leaf_size)
    block_index = jnp.arange(leaf_count, dtype=jnp.int32) + HW + band_offsets
    picked = jnp.take(blocks_all, block_index, axis=1)
    own_term = jnp.einsum(
        "lpq,slq->slp", band_blocks[:, 0], leaves, preferred_element_type=jnp.float32
    )
    partner_term = jnp.einsum(
        "lpq,slq->slp", band_blocks[:, 1], picked, preferred_element_type=jnp.float32
    )
    return (far_term + own_term + partner_term).reshape(rhs_count, point_count)


def solution(mesh):
    return jax.shard_map(
        local,
        mesh=mesh,
        in_specs=(
            P(None, ("gx", "gy")),
            P(("gx", "gy")),
            P(("gx", "gy")),
            P(("gx", "gy"), None, None),
            P(("gx", "gy"), None, None, None),
            P(("gx", "gy"), None, None, None, None, None),
            P(("gx", "gy"), None, None),
        ),
        out_specs=P(None, ("gx", "gy")),
        check_vma=False,
    )
```

```python
import jax
import jax.numpy as jnp
from jax import lax
from jax.experimental import pallas as pl
from jax.experimental.pallas import tpu as pltpu
from jax.sharding import PartitionSpec as P

HW = 16


ROWS = 32


def gather_kernel(idx_ref, x_ref, o_ref):
    def body(i, carry):
        base = pl.multiple_of(i * ROWS, ROWS)
        for g in range(ROWS // 8):
            rows = [x_ref[pl.ds(idx_ref[base + g * 8 + u], 1), :] for u in range(8)]
            o_ref[pl.ds(pl.multiple_of(base + g * 8, 8), 8), :] = jnp.concatenate(rows, axis=0)
        return carry

    lax.fori_loop(0, o_ref.shape[0] // ROWS, body, 0)


def row_gather(rows, index):
    count, width = rows.shape
    return pl.pallas_call(
        gather_kernel,
        out_shape=jax.ShapeDtypeStruct((count, width), rows.dtype),
        in_specs=[pl.BlockSpec(memory_space=pltpu.SMEM), pl.BlockSpec(memory_space=pltpu.VMEM)],
        out_specs=pl.BlockSpec(memory_space=pltpu.VMEM),
        compiler_params=pltpu.CompilerParams(vmem_limit_bytes=40 * 1024 * 1024),
        cost_estimate=pl.CostEstimate(flops=0, transcendentals=0, bytes_accessed=2 * count * width * 4),
    )(index, rows)


def from_partner(x, axis, distance):
    return lax.ppermute(x, axis, [(i, i ^ 1 << distance) for i in range(lax.axis_size(axis))])


def extended(x, sides, width):
    for axis, dim in sides:
        count, length = (lax.axis_size(axis), x.shape[dim])
        up = [(i, (i + 1) % count) for i in range(count - 1)]
        down = [(j, i) for i, j in up]
        last = lax.slice_in_dim(x, length - width, length, axis=dim)
        initial = lax.slice_in_dim(x, 0, width, axis=dim)
        before = lax.ppermute(last, axis, up)
        after = lax.ppermute(initial, axis, down)
        x = jnp.concatenate([before, x, after], axis=dim)
    return x


def translate(level_weights, own_coeffs, other_coeffs):
    first = jnp.einsum(
        "gab,bgm->agm",
        level_weights[:, 0],
        own_coeffs,
        precision=lax.Precision.HIGHEST,
        preferred_element_type=jnp.float32,
    )
    second = jnp.einsum(
        "gab,bgm->agm",
        level_weights[:, 1],
        other_coeffs,
        precision=lax.Precision.HIGHEST,
        preferred_element_type=jnp.float32,
    )
    return first + second


NODE_AXES = ("gx", "gy")


def node_partner(x, mask):
    count = lax.axis_size(NODE_AXES)
    return lax.ppermute(x, NODE_AXES, [(i, i ^ mask) for i in range(count)])


def chain(left, right):
    return jnp.einsum(
        "gab,gbc->gac", left, right, precision=lax.Precision.HIGHEST, preferred_element_type=jnp.float32
    )


def apply(matrix, values):
    return jnp.einsum(
        "gab,bgm->agm", matrix, values, precision=lax.Precision.HIGHEST, preferred_element_type=jnp.float32
    )


def two_levels(weights, first, coeffs):
    near, far = 1 << first, 1 << (first + 1)
    lower, upper = weights[first], weights[first + 1]
    lower_far = node_partner(lower, far)
    terms = (
        (chain(upper[:, 0], lower[:, 0]), 0),
        (chain(upper[:, 0], lower[:, 1]), near),
        (chain(upper[:, 1], lower_far[:, 0]), far),
        (chain(upper[:, 1], lower_far[:, 1]), near | far),
    )
    total = None
    for matrix, mask in terms:
        values = coeffs if mask == 0 else node_partner(coeffs, mask)
        term = apply(matrix, values)
        total = term if total is None else total + term
    return total


def local(points_rhs, morton_order, band_offsets, leaf_basis, band_blocks, translations, out_basis):
    rhs_count, point_count = points_rhs.shape
    leaf_count, rank_size, leaf_size = leaf_basis.shape
    group_total = translations.shape[2]
    total_cols = leaf_count * rhs_count
    group_width = total_cols // group_total
    ordered = row_gather(points_rhs.T, morton_order).T.astype(jnp.bfloat16)
    leaves = ordered.reshape(rhs_count, leaf_count, leaf_size)
    coeffs = jnp.einsum(
        "lrp,slp->rls", leaf_basis, leaves, preferred_element_type=jnp.float32
    ).reshape(rank_size, total_cols)
    weights = translations[0]
    level_count = weights.shape[0]
    coeffs = coeffs.reshape(rank_size, group_total, group_width)
    for first in range(0, level_count - 1, 2):
        coeffs = two_levels(weights, first, coeffs)
    if level_count % 2:
        partner = node_partner(coeffs, 1 << (level_count - 1))
        coeffs = translate(weights[level_count - 1], coeffs, partner)
    coeffs = coeffs.reshape(rank_size, total_cols)
    coeff_bf = coeffs.astype(jnp.bfloat16).reshape(rank_size, leaf_count, rhs_count)
    far_term = jnp.einsum("lrp,rls->slp", out_basis, coeff_bf, preferred_element_type=jnp.float32)
    padded = extended(ordered, ((("gx", "gy"), 1),), HW * leaf_size)
    blocks_all = padded.reshape(rhs_count, leaf_count + 2 * HW, leaf_size)
    block_index = jnp.arange(leaf_count, dtype=jnp.int32) + HW + band_offsets
    picked = jnp.take(blocks_all, block_index, axis=1)
    own_term = jnp.einsum(
        "lpq,slq->slp", band_blocks[:, 0], leaves, preferred_element_type=jnp.float32
    )
    partner_term = jnp.einsum(
        "lpq,slq->slp", band_blocks[:, 1], picked, preferred_element_type=jnp.float32
    )
    return (far_term + own_term + partner_term).reshape(rhs_count, point_count)


def solution(mesh):
    return jax.shard_map(
        local,
        mesh=mesh,
        in_specs=(
            P(None, ("gx", "gy")),
            P(("gx", "gy")),
            P(("gx", "gy")),
            P(("gx", "gy"), None, None),
            P(("gx", "gy"), None, None, None),
            P(("gx", "gy"), None, None, None, None, None),
            P(("gx", "gy"), None, None),
        ),
        out_specs=P(None, ("gx", "gy")),
        check_vma=False,
    )
```

```python
import jax
import jax.numpy as jnp
from jax import lax
from jax.experimental import pallas as pl
from jax.experimental.pallas import tpu as pltpu
from jax.sharding import PartitionSpec as P

HW = 16


ROWS = 32


def gather_kernel(idx_ref, x_ref, o_ref):
    def body(i, carry):
        base = pl.multiple_of(i * ROWS, ROWS)
        for g in range(ROWS // 8):
            rows = [x_ref[pl.ds(idx_ref[base + g * 8 + u], 1), :] for u in range(8)]
            o_ref[pl.ds(pl.multiple_of(base + g * 8, 8), 8), :] = jnp.concatenate(rows, axis=0)
        return carry

    lax.fori_loop(0, o_ref.shape[0] // ROWS, body, 0)


def row_gather(rows, index):
    count, width = rows.shape
    return pl.pallas_call(
        gather_kernel,
        out_shape=jax.ShapeDtypeStruct((count, width), rows.dtype),
        in_specs=[pl.BlockSpec(memory_space=pltpu.SMEM), pl.BlockSpec(memory_space=pltpu.VMEM)],
        out_specs=pl.BlockSpec(memory_space=pltpu.VMEM),
        compiler_params=pltpu.CompilerParams(vmem_limit_bytes=40 * 1024 * 1024),
        cost_estimate=pl.CostEstimate(flops=0, transcendentals=0, bytes_accessed=2 * count * width * 4),
    )(index, rows)


def from_partner(x, axis, distance):
    return lax.ppermute(x, axis, [(i, i ^ 1 << distance) for i in range(lax.axis_size(axis))])


def extended(x, sides, width):
    for axis, dim in sides:
        count, length = (lax.axis_size(axis), x.shape[dim])
        up = [(i, (i + 1) % count) for i in range(count - 1)]
        down = [(j, i) for i, j in up]
        last = lax.slice_in_dim(x, length - width, length, axis=dim)
        initial = lax.slice_in_dim(x, 0, width, axis=dim)
        before = lax.ppermute(last, axis, up)
        after = lax.ppermute(initial, axis, down)
        x = jnp.concatenate([before, x, after], axis=dim)
    return x


def translate(level_weights, own_coeffs, other_coeffs):
    first = jnp.einsum(
        "gab,bgm->agm",
        level_weights[:, 0],
        own_coeffs,
        precision=lax.Precision.HIGHEST,
        preferred_element_type=jnp.float32,
    )
    second = jnp.einsum(
        "gab,bgm->agm",
        level_weights[:, 1],
        other_coeffs,
        precision=lax.Precision.HIGHEST,
        preferred_element_type=jnp.float32,
    )
    return first + second


def near_piece(own_blocks, own_leaves, other_blocks, other_leaves):
    own = jnp.einsum("lpq,slq->slp", own_blocks, own_leaves, preferred_element_type=jnp.float32)
    other = jnp.einsum("lpq,slq->slp", other_blocks, other_leaves, preferred_element_type=jnp.float32)
    return own + other


def local(points_rhs, morton_order, band_offsets, leaf_basis, band_blocks, translations, out_basis):
    rhs_count, point_count = points_rhs.shape
    leaf_count, rank_size, leaf_size = leaf_basis.shape
    group_total = translations.shape[2]
    total_cols = leaf_count * rhs_count
    group_width = total_cols // group_total
    ordered = row_gather(points_rhs.T, morton_order).T.astype(jnp.bfloat16)
    leaves = ordered.reshape(rhs_count, leaf_count, leaf_size)
    padded = extended(ordered, ((("gx", "gy"), 1),), HW * leaf_size)
    coeffs = jnp.einsum(
        "lrp,slp->rls", leaf_basis, leaves, preferred_element_type=jnp.float32
    ).reshape(rank_size, total_cols)
    weights = translations[0]
    low_bits = lax.axis_size("gy").bit_length() - 1
    high_bits = lax.axis_size("gx").bit_length() - 1
    levels = [("gy", bit, bit) for bit in range(low_bits)]
    levels += [("gx", bit, low_bits + bit) for bit in range(high_bits)]
    pieces = len(levels)
    bounds = [leaf_count * k // pieces for k in range(pieces + 1)]
    blocks_all = padded.reshape(rhs_count, leaf_count + 2 * HW, leaf_size)
    block_index = jnp.arange(leaf_count, dtype=jnp.int32) + HW + band_offsets
    coeffs = coeffs.reshape(rank_size, group_total, group_width)
    near_parts = []
    for piece, (axis, bit, level) in enumerate(levels):
        low, high = bounds[piece], bounds[piece + 1]
        coeffs, piece_leaves, piece_index = lax.optimization_barrier(
            (coeffs, leaves[:, low:high], block_index[low:high])
        )
        partner = from_partner(coeffs, axis, bit)
        picked = jnp.take(blocks_all, piece_index, axis=1)
        near_parts.append(
            near_piece(band_blocks[low:high, 0], piece_leaves, band_blocks[low:high, 1], picked)
        )
        coeffs = translate(weights[level], coeffs, partner)
    coeffs = coeffs.reshape(rank_size, total_cols)
    coeff_bf = coeffs.astype(jnp.bfloat16).reshape(rank_size, leaf_count, rhs_count)
    far_term = jnp.einsum("lrp,rls->slp", out_basis, coeff_bf, preferred_element_type=jnp.float32)
    near_term = jnp.concatenate(near_parts, axis=1)
    return (far_term + near_term).reshape(rhs_count, point_count)


def solution(mesh):
    return jax.shard_map(
        local,
        mesh=mesh,
        in_specs=(
            P(None, ("gx", "gy")),
            P(("gx", "gy")),
            P(("gx", "gy")),
            P(("gx", "gy"), None, None),
            P(("gx", "gy"), None, None, None),
            P(("gx", "gy"), None, None, None, None, None),
            P(("gx", "gy"), None, None),
        ),
        out_specs=P(None, ("gx", "gy")),
        check_vma=False,
    )
```

```python
import jax
import jax.numpy as jnp
from jax import lax
from jax.experimental import pallas as pl
from jax.experimental.pallas import tpu as pltpu
from jax.sharding import PartitionSpec as P

HW = 16


CHUNK = 128


def gather_kernel(idx_ref, x_ref, o_ref, xt_ref):
    count = o_ref.shape[1]

    def spread(c, carry):
        col = pl.multiple_of(c * CHUNK, CHUNK)
        xt_ref[pl.ds(col, CHUNK), :] = x_ref[:, pl.ds(col, CHUNK)].T
        return carry

    lax.fori_loop(0, count // CHUNK, spread, 0)

    def body(c, carry):
        col = pl.multiple_of(c * CHUNK, CHUNK)
        rows = [xt_ref[pl.ds(idx_ref[col + u], 1), :] for u in range(CHUNK)]
        o_ref[:, pl.ds(col, CHUNK)] = jnp.concatenate(rows, axis=0).T.astype(o_ref.dtype)
        return carry

    lax.fori_loop(0, count // CHUNK, body, 0)


def gather_points(points, index):
    width, count = points.shape
    return pl.pallas_call(
        gather_kernel,
        out_shape=jax.ShapeDtypeStruct((width, count), jnp.bfloat16),
        in_specs=[pl.BlockSpec(memory_space=pltpu.SMEM), pl.BlockSpec(memory_space=pltpu.VMEM)],
        out_specs=pl.BlockSpec(memory_space=pltpu.VMEM),
        scratch_shapes=[pltpu.VMEM((count, width), jnp.float32)],
        compiler_params=pltpu.CompilerParams(vmem_limit_bytes=40 * 1024 * 1024),
        cost_estimate=pl.CostEstimate(flops=0, transcendentals=0, bytes_accessed=count * width * 6),
    )(index, points)


def from_partner(x, axis, distance):
    return lax.ppermute(x, axis, [(i, i ^ 1 << distance) for i in range(lax.axis_size(axis))])


def extended(x, sides, width):
    for axis, dim in sides:
        count, length = (lax.axis_size(axis), x.shape[dim])
        up = [(i, (i + 1) % count) for i in range(count - 1)]
        down = [(j, i) for i, j in up]
        last = lax.slice_in_dim(x, length - width, length, axis=dim)
        initial = lax.slice_in_dim(x, 0, width, axis=dim)
        before = lax.ppermute(last, axis, up)
        after = lax.ppermute(initial, axis, down)
        x = jnp.concatenate([before, x, after], axis=dim)
    return x


def translate(level_weights, own_coeffs, other_coeffs):
    first = jnp.einsum(
        "gab,bgm->agm",
        level_weights[:, 0],
        own_coeffs,
        precision=lax.Precision.HIGHEST,
        preferred_element_type=jnp.float32,
    )
    second = jnp.einsum(
        "gab,bgm->agm",
        level_weights[:, 1],
        other_coeffs,
        precision=lax.Precision.HIGHEST,
        preferred_element_type=jnp.float32,
    )
    return first + second


def local(points_rhs, morton_order, band_offsets, leaf_basis, band_blocks, translations, out_basis):
    rhs_count, point_count = points_rhs.shape
    leaf_count, rank_size, leaf_size = leaf_basis.shape
    group_total = translations.shape[2]
    total_cols = leaf_count * rhs_count
    group_width = total_cols // group_total
    ordered = gather_points(points_rhs, morton_order)
    leaves = ordered.reshape(rhs_count, leaf_count, leaf_size)
    coeffs = jnp.einsum(
        "lrp,slp->rls", leaf_basis, leaves, preferred_element_type=jnp.float32
    ).reshape(rank_size, total_cols)
    weights = translations[0]
    low_bits = lax.axis_size("gy").bit_length() - 1
    high_bits = lax.axis_size("gx").bit_length() - 1
    coeffs = coeffs.reshape(rank_size, group_total, group_width)
    for level_bit in range(low_bits):
        partner = from_partner(coeffs, "gy", level_bit)
        coeffs = translate(weights[level_bit], coeffs, partner)
    for level_bit in range(high_bits):
        partner = from_partner(coeffs, "gx", level_bit)
        coeffs = translate(weights[low_bits + level_bit], coeffs, partner)
    coeffs = coeffs.reshape(rank_size, total_cols)
    coeff_bf = coeffs.astype(jnp.bfloat16).reshape(rank_size, leaf_count, rhs_count)
    far_term = jnp.einsum("lrp,rls->slp", out_basis, coeff_bf, preferred_element_type=jnp.float32)
    padded = extended(ordered, ((("gx", "gy"), 1),), HW * leaf_size)
    blocks_all = padded.reshape(rhs_count, leaf_count + 2 * HW, leaf_size)
    block_index = jnp.arange(leaf_count, dtype=jnp.int32) + HW + band_offsets
    picked = jnp.take(blocks_all, block_index, axis=1)
    own_term = jnp.einsum(
        "lpq,slq->slp", band_blocks[:, 0], leaves, preferred_element_type=jnp.float32
    )
    partner_term = jnp.einsum(
        "lpq,slq->slp", band_blocks[:, 1], picked, preferred_element_type=jnp.float32
    )
    return (far_term + own_term + partner_term).reshape(rhs_count, point_count)


def solution(mesh):
    return jax.shard_map(
        local,
        mesh=mesh,
        in_specs=(
            P(None, ("gx", "gy")),
            P(("gx", "gy")),
            P(("gx", "gy")),
            P(("gx", "gy"), None, None),
            P(("gx", "gy"), None, None, None),
            P(("gx", "gy"), None, None, None, None, None),
            P(("gx", "gy"), None, None),
        ),
        out_specs=P(None, ("gx", "gy")),
        check_vma=False,
    )
```

```python
import jax
import jax.numpy as jnp
from jax import lax
from jax.experimental import pallas as pl
from jax.experimental.pallas import tpu as pltpu
from jax.sharding import PartitionSpec as P

HW = 16


CHUNK = 128


def gather_kernel(idx_ref, x_ref, o_ref, xt_ref):
    count = o_ref.shape[1]

    def spread(c, carry):
        col = pl.multiple_of(c * CHUNK, CHUNK)
        xt_ref[pl.ds(col, CHUNK), :] = x_ref[:, pl.ds(col, CHUNK)].T
        return carry

    lax.fori_loop(0, count // CHUNK, spread, 0)

    def body(c, carry):
        col = pl.multiple_of(c * CHUNK, CHUNK)
        rows = [xt_ref[pl.ds(idx_ref[col + u], 1), :] for u in range(CHUNK)]
        o_ref[:, pl.ds(col, CHUNK)] = jnp.concatenate(rows, axis=0).T.astype(o_ref.dtype)
        return carry

    lax.fori_loop(0, count // CHUNK, body, 0)


def gather_points(points, index):
    width, count = points.shape
    return pl.pallas_call(
        gather_kernel,
        out_shape=jax.ShapeDtypeStruct((width, count), jnp.bfloat16),
        in_specs=[pl.BlockSpec(memory_space=pltpu.SMEM), pl.BlockSpec(memory_space=pltpu.VMEM)],
        out_specs=pl.BlockSpec(memory_space=pltpu.VMEM),
        scratch_shapes=[pltpu.VMEM((count, width), jnp.float32)],
        compiler_params=pltpu.CompilerParams(vmem_limit_bytes=40 * 1024 * 1024),
        cost_estimate=pl.CostEstimate(flops=0, transcendentals=0, bytes_accessed=count * width * 6),
    )(index, points)


def from_partner(x, axis, distance):
    return lax.ppermute(x, axis, [(i, i ^ 1 << distance) for i in range(lax.axis_size(axis))])


def extended(x, sides, width):
    for axis, dim in sides:
        count, length = (lax.axis_size(axis), x.shape[dim])
        up = [(i, (i + 1) % count) for i in range(count - 1)]
        down = [(j, i) for i, j in up]
        last = lax.slice_in_dim(x, length - width, length, axis=dim)
        initial = lax.slice_in_dim(x, 0, width, axis=dim)
        before = lax.ppermute(last, axis, up)
        after = lax.ppermute(initial, axis, down)
        x = jnp.concatenate([before, x, after], axis=dim)
    return x


def translate(level_weights, own_coeffs, other_coeffs):
    first = jnp.einsum(
        "gab,bgm->agm",
        level_weights[:, 0],
        own_coeffs,
        precision=lax.Precision.HIGH,
        preferred_element_type=jnp.float32,
    )
    second = jnp.einsum(
        "gab,bgm->agm",
        level_weights[:, 1],
        other_coeffs,
        precision=lax.Precision.HIGH,
        preferred_element_type=jnp.float32,
    )
    return first + second


def local(points_rhs, morton_order, band_offsets, leaf_basis, band_blocks, translations, out_basis):
    rhs_count, point_count = points_rhs.shape
    leaf_count, rank_size, leaf_size = leaf_basis.shape
    group_total = translations.shape[2]
    total_cols = leaf_count * rhs_count
    group_width = total_cols // group_total
    ordered = gather_points(points_rhs, morton_order)
    leaves = ordered.reshape(rhs_count, leaf_count, leaf_size)
    coeffs = jnp.einsum(
        "lrp,slp->rls", leaf_basis, leaves, preferred_element_type=jnp.float32
    ).reshape(rank_size, total_cols)
    weights = translations[0]
    low_bits = lax.axis_size("gy").bit_length() - 1
    high_bits = lax.axis_size("gx").bit_length() - 1
    coeffs = coeffs.reshape(rank_size, group_total, group_width)
    for level_bit in range(low_bits):
        partner = from_partner(coeffs, "gy", level_bit)
        coeffs = translate(weights[level_bit], coeffs, partner)
    for level_bit in range(high_bits):
        partner = from_partner(coeffs, "gx", level_bit)
        coeffs = translate(weights[low_bits + level_bit], coeffs, partner)
    coeffs = coeffs.reshape(rank_size, total_cols)
    coeff_bf = coeffs.astype(jnp.bfloat16).reshape(rank_size, leaf_count, rhs_count)
    far_term = jnp.einsum("lrp,rls->slp", out_basis, coeff_bf, preferred_element_type=jnp.float32)
    padded = extended(ordered, ((("gx", "gy"), 1),), HW * leaf_size)
    blocks_all = padded.reshape(rhs_count, leaf_count + 2 * HW, leaf_size)
    block_index = jnp.arange(leaf_count, dtype=jnp.int32) + HW + band_offsets
    picked = jnp.take(blocks_all, block_index, axis=1)
    own_term = jnp.einsum(
        "lpq,slq->slp", band_blocks[:, 0], leaves, preferred_element_type=jnp.float32
    )
    partner_term = jnp.einsum(
        "lpq,slq->slp", band_blocks[:, 1], picked, preferred_element_type=jnp.float32
    )
    return (far_term + own_term + partner_term).reshape(rhs_count, point_count)


def solution(mesh):
    return jax.shard_map(
        local,
        mesh=mesh,
        in_specs=(
            P(None, ("gx", "gy")),
            P(("gx", "gy")),
            P(("gx", "gy")),
            P(("gx", "gy"), None, None),
            P(("gx", "gy"), None, None, None),
            P(("gx", "gy"), None, None, None, None, None),
            P(("gx", "gy"), None, None),
        ),
        out_specs=P(None, ("gx", "gy")),
        check_vma=False,
    )
```

```python
import jax
import jax.numpy as jnp
from jax import lax
from jax.experimental import pallas as pl
from jax.experimental.pallas import tpu as pltpu
from jax.sharding import PartitionSpec as P

HW = 16


CHUNK = 128


def gather_kernel(idx_ref, x_ref, o_ref, xt_ref):
    count = o_ref.shape[1]

    def spread(c, carry):
        col = pl.multiple_of(c * CHUNK, CHUNK)
        xt_ref[pl.ds(col, CHUNK), :] = x_ref[:, pl.ds(col, CHUNK)].T
        return carry

    lax.fori_loop(0, count // CHUNK, spread, 0)

    def body(c, carry):
        col = pl.multiple_of(c * CHUNK, CHUNK)
        rows = [xt_ref[pl.ds(idx_ref[col + u], 1), :] for u in range(CHUNK)]
        o_ref[:, pl.ds(col, CHUNK)] = jnp.concatenate(rows, axis=0).T.astype(o_ref.dtype)
        return carry

    lax.fori_loop(0, count // CHUNK, body, 0)


def gather_points(points, index):
    width, count = points.shape
    return pl.pallas_call(
        gather_kernel,
        out_shape=jax.ShapeDtypeStruct((width, count), jnp.bfloat16),
        in_specs=[pl.BlockSpec(memory_space=pltpu.SMEM), pl.BlockSpec(memory_space=pltpu.VMEM)],
        out_specs=pl.BlockSpec(memory_space=pltpu.VMEM),
        scratch_shapes=[pltpu.VMEM((count, width), jnp.float32)],
        compiler_params=pltpu.CompilerParams(vmem_limit_bytes=40 * 1024 * 1024),
        cost_estimate=pl.CostEstimate(flops=0, transcendentals=0, bytes_accessed=count * width * 6),
    )(index, points)


def from_partner(x, axis, distance):
    return lax.ppermute(x, axis, [(i, i ^ 1 << distance) for i in range(lax.axis_size(axis))])


def extended(x, sides, width):
    for axis, dim in sides:
        count, length = (lax.axis_size(axis), x.shape[dim])
        up = [(i, (i + 1) % count) for i in range(count - 1)]
        down = [(j, i) for i, j in up]
        last = lax.slice_in_dim(x, length - width, length, axis=dim)
        initial = lax.slice_in_dim(x, 0, width, axis=dim)
        before = lax.ppermute(last, axis, up)
        after = lax.ppermute(initial, axis, down)
        x = jnp.concatenate([before, x, after], axis=dim)
    return x


def block_diagonal(blocks):
    groups, rank, _ = blocks.shape
    eye = jnp.eye(groups, dtype=blocks.dtype)
    spread = eye[:, None, :, None] * blocks[:, :, None, :]
    return spread.reshape(groups * rank, groups * rank)


def translate(level_weights, own_coeffs, other_coeffs):
    first = jnp.dot(
        block_diagonal(level_weights[:, 0]),
        own_coeffs,
        precision=lax.Precision.HIGHEST,
        preferred_element_type=jnp.float32,
    )
    second = jnp.dot(
        block_diagonal(level_weights[:, 1]),
        other_coeffs,
        precision=lax.Precision.HIGHEST,
        preferred_element_type=jnp.float32,
    )
    return first + second


def local(points_rhs, morton_order, band_offsets, leaf_basis, band_blocks, translations, out_basis):
    rhs_count, point_count = points_rhs.shape
    leaf_count, rank_size, leaf_size = leaf_basis.shape
    group_total = translations.shape[2]
    total_cols = leaf_count * rhs_count
    group_width = total_cols // group_total
    ordered = gather_points(points_rhs, morton_order)
    leaves = ordered.reshape(rhs_count, leaf_count, leaf_size)
    coeffs = jnp.einsum(
        "lrp,slp->rls", leaf_basis, leaves, preferred_element_type=jnp.float32
    ).reshape(rank_size, total_cols)
    weights = translations[0]
    low_bits = lax.axis_size("gy").bit_length() - 1
    high_bits = lax.axis_size("gx").bit_length() - 1
    coeffs = coeffs.reshape(rank_size, group_total, group_width).transpose(1, 0, 2)
    coeffs = coeffs.reshape(group_total * rank_size, group_width)
    for level_bit in range(low_bits):
        partner = from_partner(coeffs, "gy", level_bit)
        coeffs = translate(weights[level_bit], coeffs, partner)
    for level_bit in range(high_bits):
        partner = from_partner(coeffs, "gx", level_bit)
        coeffs = translate(weights[low_bits + level_bit], coeffs, partner)
    coeffs = coeffs.reshape(group_total, rank_size, group_width).transpose(1, 0, 2)
    coeffs = coeffs.reshape(rank_size, total_cols)
    coeff_bf = coeffs.astype(jnp.bfloat16).reshape(rank_size, leaf_count, rhs_count)
    far_term = jnp.einsum("lrp,rls->slp", out_basis, coeff_bf, preferred_element_type=jnp.float32)
    padded = extended(ordered, ((("gx", "gy"), 1),), HW * leaf_size)
    blocks_all = padded.reshape(rhs_count, leaf_count + 2 * HW, leaf_size)
    block_index = jnp.arange(leaf_count, dtype=jnp.int32) + HW + band_offsets
    picked = jnp.take(blocks_all, block_index, axis=1)
    own_term = jnp.einsum(
        "lpq,slq->slp", band_blocks[:, 0], leaves, preferred_element_type=jnp.float32
    )
    partner_term = jnp.einsum(
        "lpq,slq->slp", band_blocks[:, 1], picked, preferred_element_type=jnp.float32
    )
    return (far_term + own_term + partner_term).reshape(rhs_count, point_count)


def solution(mesh):
    return jax.shard_map(
        local,
        mesh=mesh,
        in_specs=(
            P(None, ("gx", "gy")),
            P(("gx", "gy")),
            P(("gx", "gy")),
            P(("gx", "gy"), None, None),
            P(("gx", "gy"), None, None, None),
            P(("gx", "gy"), None, None, None, None, None),
            P(("gx", "gy"), None, None),
        ),
        out_specs=P(None, ("gx", "gy")),
        check_vma=False,
    )
```

```python
import jax
import jax.numpy as jnp
from jax import lax
from jax.experimental import pallas as pl
from jax.experimental.pallas import tpu as pltpu
from jax.sharding import PartitionSpec as P

HW = 16


CHUNK = 128


def gather_kernel(idx_ref, x_ref, o_ref, xt_ref):
    count = o_ref.shape[1]

    def spread(c, carry):
        col = pl.multiple_of(c * CHUNK, CHUNK)
        xt_ref[pl.ds(col, CHUNK), :] = x_ref[:, pl.ds(col, CHUNK)].T
        return carry

    lax.fori_loop(0, count // CHUNK, spread, 0)

    def body(c, carry):
        col = pl.multiple_of(c * CHUNK, CHUNK)
        rows = [xt_ref[pl.ds(idx_ref[col + u], 1), :] for u in range(CHUNK)]
        o_ref[:, pl.ds(col, CHUNK)] = jnp.concatenate(rows, axis=0).T.astype(o_ref.dtype)
        return carry

    lax.fori_loop(0, count // CHUNK, body, 0)


def gather_points(points, index):
    width, count = points.shape
    return pl.pallas_call(
        gather_kernel,
        out_shape=jax.ShapeDtypeStruct((width, count), jnp.bfloat16),
        in_specs=[pl.BlockSpec(memory_space=pltpu.SMEM), pl.BlockSpec(memory_space=pltpu.VMEM)],
        out_specs=pl.BlockSpec(memory_space=pltpu.VMEM),
        scratch_shapes=[pltpu.VMEM((count, width), jnp.float32)],
        compiler_params=pltpu.CompilerParams(vmem_limit_bytes=40 * 1024 * 1024),
        cost_estimate=pl.CostEstimate(flops=0, transcendentals=0, bytes_accessed=count * width * 6),
    )(index, points)


def from_partner(x, axis, distance):
    return lax.ppermute(x, axis, [(i, i ^ 1 << distance) for i in range(lax.axis_size(axis))])


def extended(x, sides, width):
    for axis, dim in sides:
        count, length = (lax.axis_size(axis), x.shape[dim])
        up = [(i, (i + 1) % count) for i in range(count - 1)]
        down = [(j, i) for i, j in up]
        last = lax.slice_in_dim(x, length - width, length, axis=dim)
        initial = lax.slice_in_dim(x, 0, width, axis=dim)
        before = lax.ppermute(last, axis, up)
        after = lax.ppermute(initial, axis, down)
        x = jnp.concatenate([before, x, after], axis=dim)
    return x


def block_diagonals(weights):
    levels, groups, terms, rank, _ = weights.shape
    width = groups * rank
    shape = (groups, rank, width)
    target = lax.broadcasted_iota(jnp.int32, shape, 0) * rank + lax.broadcasted_iota(jnp.int32, shape, 1)
    spread = (lax.broadcasted_iota(jnp.int32, shape, 2) == target).astype(weights.dtype)
    return jnp.einsum(
        "lgtab,gbc->ltgac", weights, spread, precision=lax.Precision.HIGHEST, preferred_element_type=jnp.float32
    ).reshape(levels, terms, width, width)


def translate(level_matrices, own_coeffs, other_coeffs):
    first = jnp.dot(
        level_matrices[0],
        own_coeffs,
        precision=lax.Precision.HIGHEST,
        preferred_element_type=jnp.float32,
    )
    second = jnp.dot(
        level_matrices[1],
        other_coeffs,
        precision=lax.Precision.HIGHEST,
        preferred_element_type=jnp.float32,
    )
    return first + second


def local(points_rhs, morton_order, band_offsets, leaf_basis, band_blocks, translations, out_basis):
    rhs_count, point_count = points_rhs.shape
    leaf_count, rank_size, leaf_size = leaf_basis.shape
    group_total = translations.shape[2]
    total_cols = leaf_count * rhs_count
    group_width = total_cols // group_total
    ordered = gather_points(points_rhs, morton_order)
    leaves = ordered.reshape(rhs_count, leaf_count, leaf_size)
    coeffs = jnp.einsum(
        "lrp,slp->rls", leaf_basis, leaves, preferred_element_type=jnp.float32
    ).reshape(rank_size, total_cols)
    weights = block_diagonals(translations[0])
    low_bits = lax.axis_size("gy").bit_length() - 1
    high_bits = lax.axis_size("gx").bit_length() - 1
    coeffs = coeffs.reshape(rank_size, group_total, group_width).transpose(1, 0, 2)
    coeffs = coeffs.reshape(group_total * rank_size, group_width)
    for level_bit in range(low_bits):
        partner = from_partner(coeffs, "gy", level_bit)
        coeffs = translate(weights[level_bit], coeffs, partner)
    for level_bit in range(high_bits):
        partner = from_partner(coeffs, "gx", level_bit)
        coeffs = translate(weights[low_bits + level_bit], coeffs, partner)
    coeffs = coeffs.reshape(group_total, rank_size, group_width).transpose(1, 0, 2)
    coeffs = coeffs.reshape(rank_size, total_cols)
    coeff_bf = coeffs.astype(jnp.bfloat16).reshape(rank_size, leaf_count, rhs_count)
    far_term = jnp.einsum("lrp,rls->slp", out_basis, coeff_bf, preferred_element_type=jnp.float32)
    padded = extended(ordered, ((("gx", "gy"), 1),), HW * leaf_size)
    blocks_all = padded.reshape(rhs_count, leaf_count + 2 * HW, leaf_size)
    block_index = jnp.arange(leaf_count, dtype=jnp.int32) + HW + band_offsets
    picked = jnp.take(blocks_all, block_index, axis=1)
    own_term = jnp.einsum(
        "lpq,slq->slp", band_blocks[:, 0], leaves, preferred_element_type=jnp.float32
    )
    partner_term = jnp.einsum(
        "lpq,slq->slp", band_blocks[:, 1], picked, preferred_element_type=jnp.float32
    )
    return (far_term + own_term + partner_term).reshape(rhs_count, point_count)


def solution(mesh):
    return jax.shard_map(
        local,
        mesh=mesh,
        in_specs=(
            P(None, ("gx", "gy")),
            P(("gx", "gy")),
            P(("gx", "gy")),
            P(("gx", "gy"), None, None),
            P(("gx", "gy"), None, None, None),
            P(("gx", "gy"), None, None, None, None, None),
            P(("gx", "gy"), None, None),
        ),
        out_specs=P(None, ("gx", "gy")),
        check_vma=False,
    )
```

```python
import jax
import jax.numpy as jnp
from jax import lax
from jax.experimental import pallas as pl
from jax.experimental.pallas import tpu as pltpu
from jax.sharding import PartitionSpec as P

HW = 16


CHUNK = 128


def gather_kernel(idx_ref, x_ref, o_ref, xt_ref):
    count = o_ref.shape[1]

    def spread(c, carry):
        col = pl.multiple_of(c * CHUNK, CHUNK)
        xt_ref[pl.ds(col, CHUNK), :] = x_ref[:, pl.ds(col, CHUNK)].T
        return carry

    lax.fori_loop(0, count // CHUNK, spread, 0)

    def body(c, carry):
        col = pl.multiple_of(c * CHUNK, CHUNK)
        rows = [xt_ref[pl.ds(idx_ref[col + u], 1), :] for u in range(CHUNK)]
        o_ref[:, pl.ds(col, CHUNK)] = jnp.concatenate(rows, axis=0).T.astype(o_ref.dtype)
        return carry

    lax.fori_loop(0, count // CHUNK, body, 0)


def gather_points(points, index):
    width, count = points.shape
    return pl.pallas_call(
        gather_kernel,
        out_shape=jax.ShapeDtypeStruct((width, count), jnp.bfloat16),
        in_specs=[pl.BlockSpec(memory_space=pltpu.SMEM), pl.BlockSpec(memory_space=pltpu.VMEM)],
        out_specs=pl.BlockSpec(memory_space=pltpu.VMEM),
        scratch_shapes=[pltpu.VMEM((count, width), jnp.float32)],
        compiler_params=pltpu.CompilerParams(vmem_limit_bytes=40 * 1024 * 1024),
        cost_estimate=pl.CostEstimate(flops=0, transcendentals=0, bytes_accessed=count * width * 6),
    )(index, points)


def from_partner(x, axis, distance):
    return lax.ppermute(x, axis, [(i, i ^ 1 << distance) for i in range(lax.axis_size(axis))])


def extended(x, sides, width):
    for axis, dim in sides:
        count, length = (lax.axis_size(axis), x.shape[dim])
        up = [(i, (i + 1) % count) for i in range(count - 1)]
        down = [(j, i) for i, j in up]
        last = lax.slice_in_dim(x, length - width, length, axis=dim)
        initial = lax.slice_in_dim(x, 0, width, axis=dim)
        before = lax.ppermute(last, axis, up)
        after = lax.ppermute(initial, axis, down)
        x = jnp.concatenate([before, x, after], axis=dim)
    return x


def block_diagonals(weights):
    levels, groups, terms, rank, _ = weights.shape
    width = groups * rank
    shape = (groups, rank, width)
    target = lax.broadcasted_iota(jnp.int32, shape, 0) * rank + lax.broadcasted_iota(jnp.int32, shape, 1)
    spread = (lax.broadcasted_iota(jnp.int32, shape, 2) == target).astype(weights.dtype)
    return jnp.einsum(
        "lgtab,gbc->ltgac", weights, spread, precision=lax.Precision.HIGHEST, preferred_element_type=jnp.float32
    ).reshape(levels, terms, width, width)


def translate(level_matrices, own_coeffs, other_coeffs):
    first = jnp.dot(
        level_matrices[0],
        own_coeffs,
        precision=lax.Precision.HIGHEST,
        preferred_element_type=jnp.float32,
    )
    second = jnp.dot(
        level_matrices[1],
        other_coeffs,
        precision=lax.Precision.HIGHEST,
        preferred_element_type=jnp.float32,
    )
    return first + second


def local(points_rhs, morton_order, band_offsets, leaf_basis, band_blocks, translations, out_basis):
    rhs_count, point_count = points_rhs.shape
    leaf_count, rank_size, leaf_size = leaf_basis.shape
    group_total = translations.shape[2]
    total_cols = leaf_count * rhs_count
    group_width = total_cols // group_total
    ordered = gather_points(points_rhs, morton_order)
    leaves = ordered.reshape(rhs_count, leaf_count, leaf_size)
    coeffs = jnp.einsum(
        "lrp,slp->rls", leaf_basis, leaves, preferred_element_type=jnp.float32
    ).reshape(rank_size, total_cols)
    weights = block_diagonals(translations[0])
    low_bits = lax.axis_size("gy").bit_length() - 1
    high_bits = lax.axis_size("gx").bit_length() - 1
    levels = [("gy", bit) for bit in range(low_bits)] + [("gx", bit) for bit in range(high_bits)]
    own_at, partner_at = min(2, len(levels) - 1), min(4, len(levels) - 1)
    padded = extended(ordered, ((("gx", "gy"), 1),), HW * leaf_size)
    coeffs = coeffs.reshape(rank_size, group_total, group_width).transpose(1, 0, 2)
    coeffs = coeffs.reshape(group_total * rank_size, group_width)
    for level, (axis, bit) in enumerate(levels):
        if level == own_at:
            coeffs, leaves = lax.optimization_barrier((coeffs, leaves))
        if level == partner_at:
            coeffs, padded = lax.optimization_barrier((coeffs, padded))
        partner = from_partner(coeffs, axis, bit)
        coeffs = translate(weights[level], coeffs, partner)
    coeffs = coeffs.reshape(group_total, rank_size, group_width).transpose(1, 0, 2)
    coeffs = coeffs.reshape(rank_size, total_cols)
    coeff_bf = coeffs.astype(jnp.bfloat16).reshape(rank_size, leaf_count, rhs_count)
    far_term = jnp.einsum("lrp,rls->slp", out_basis, coeff_bf, preferred_element_type=jnp.float32)
    blocks_all = padded.reshape(rhs_count, leaf_count + 2 * HW, leaf_size)
    block_index = jnp.arange(leaf_count, dtype=jnp.int32) + HW + band_offsets
    picked = jnp.take(blocks_all, block_index, axis=1)
    own_term = jnp.einsum(
        "lpq,slq->slp", band_blocks[:, 0], leaves, preferred_element_type=jnp.float32
    )
    partner_term = jnp.einsum(
        "lpq,slq->slp", band_blocks[:, 1], picked, preferred_element_type=jnp.float32
    )
    return (far_term + own_term + partner_term).reshape(rhs_count, point_count)


def solution(mesh):
    return jax.shard_map(
        local,
        mesh=mesh,
        in_specs=(
            P(None, ("gx", "gy")),
            P(("gx", "gy")),
            P(("gx", "gy")),
            P(("gx", "gy"), None, None),
            P(("gx", "gy"), None, None, None),
            P(("gx", "gy"), None, None, None, None, None),
            P(("gx", "gy"), None, None),
        ),
        out_specs=P(None, ("gx", "gy")),
        check_vma=False,
    )
```

```python
import jax
import jax.numpy as jnp
from jax import lax
from jax.experimental import pallas as pl
from jax.experimental.pallas import tpu as pltpu
from jax.sharding import PartitionSpec as P

HW = 16


CHUNK = 128


def gather_kernel(idx_ref, x_ref, o_ref, xt_ref):
    count = o_ref.shape[1]

    def spread(c, carry):
        col = pl.multiple_of(c * CHUNK, CHUNK)
        xt_ref[pl.ds(col, CHUNK), :] = x_ref[:, pl.ds(col, CHUNK)].T
        return carry

    lax.fori_loop(0, count // CHUNK, spread, 0)

    def body(c, carry):
        col = pl.multiple_of(c * CHUNK, CHUNK)
        rows = [xt_ref[pl.ds(idx_ref[col + u], 1), :] for u in range(CHUNK)]
        o_ref[:, pl.ds(col, CHUNK)] = jnp.concatenate(rows, axis=0).T.astype(o_ref.dtype)
        return carry

    lax.fori_loop(0, count // CHUNK, body, 0)


def gather_points(points, index):
    width, count = points.shape
    return pl.pallas_call(
        gather_kernel,
        out_shape=jax.ShapeDtypeStruct((width, count), jnp.bfloat16),
        in_specs=[pl.BlockSpec(memory_space=pltpu.SMEM), pl.BlockSpec(memory_space=pltpu.VMEM)],
        out_specs=pl.BlockSpec(memory_space=pltpu.VMEM),
        scratch_shapes=[pltpu.VMEM((count, width), jnp.float32)],
        compiler_params=pltpu.CompilerParams(vmem_limit_bytes=40 * 1024 * 1024),
        cost_estimate=pl.CostEstimate(flops=0, transcendentals=0, bytes_accessed=count * width * 6),
    )(index, points)


def from_partner(x, axis, distance):
    return lax.ppermute(x, axis, [(i, i ^ 1 << distance) for i in range(lax.axis_size(axis))])


def extended(x, sides, width):
    for axis, dim in sides:
        count, length = (lax.axis_size(axis), x.shape[dim])
        up = [(i, (i + 1) % count) for i in range(count - 1)]
        down = [(j, i) for i, j in up]
        last = lax.slice_in_dim(x, length - width, length, axis=dim)
        initial = lax.slice_in_dim(x, 0, width, axis=dim)
        before = lax.ppermute(last, axis, up)
        after = lax.ppermute(initial, axis, down)
        x = jnp.concatenate([before, x, after], axis=dim)
    return x


def block_diagonals(weights):
    levels, groups, terms, rank, _ = weights.shape
    width = groups * rank
    shape = (groups, rank, width)
    target = lax.broadcasted_iota(jnp.int32, shape, 0) * rank + lax.broadcasted_iota(jnp.int32, shape, 1)
    spread = (lax.broadcasted_iota(jnp.int32, shape, 2) == target).astype(weights.dtype)
    return jnp.einsum(
        "lgtab,gbc->ltgac", weights, spread, precision=lax.Precision.HIGHEST, preferred_element_type=jnp.float32
    ).reshape(levels, terms, width, width)


def translate(level_matrices, own_coeffs, other_coeffs):
    first = jnp.dot(
        level_matrices[0],
        own_coeffs,
        precision=lax.Precision.HIGHEST,
        preferred_element_type=jnp.float32,
    )
    second = jnp.dot(
        level_matrices[1],
        other_coeffs,
        precision=lax.Precision.HIGHEST,
        preferred_element_type=jnp.float32,
    )
    return first + second


def local(points_rhs, morton_order, band_offsets, leaf_basis, band_blocks, translations, out_basis):
    rhs_count, point_count = points_rhs.shape
    leaf_count, rank_size, leaf_size = leaf_basis.shape
    group_total = translations.shape[2]
    total_cols = leaf_count * rhs_count
    group_width = total_cols // group_total
    ordered = gather_points(points_rhs, morton_order)
    leaves = ordered.reshape(rhs_count, leaf_count, leaf_size)
    coeffs = jnp.einsum(
        "lrp,slp->rls", leaf_basis, leaves, preferred_element_type=jnp.float32
    ).reshape(rank_size, total_cols)
    weights = block_diagonals(translations[0])
    low_bits = lax.axis_size("gy").bit_length() - 1
    high_bits = lax.axis_size("gx").bit_length() - 1
    levels = [("gy", bit) for bit in range(low_bits)] + [("gx", bit) for bit in range(high_bits)]
    last = len(levels) - 1
    take_at, own_at, first_at, second_at = (min(k, last) for k in (1, 2, 4, 5))
    padded = extended(ordered, ((("gx", "gy"), 1),), HW * leaf_size)
    blocks_all = padded.reshape(rhs_count, leaf_count + 2 * HW, leaf_size)
    block_index = jnp.arange(leaf_count, dtype=jnp.int32) + HW + band_offsets
    half = leaf_count // 2
    coeffs = coeffs.reshape(rank_size, group_total, group_width).transpose(1, 0, 2)
    coeffs = coeffs.reshape(group_total * rank_size, group_width)
    picked = None
    for level, (axis, bit) in enumerate(levels):
        if level == take_at:
            coeffs, blocks_all = lax.optimization_barrier((coeffs, blocks_all))
            picked = jnp.take(blocks_all, block_index, axis=1)
        if level == own_at:
            coeffs, leaves = lax.optimization_barrier((coeffs, leaves))
        if level == first_at:
            coeffs, picked_first = lax.optimization_barrier((coeffs, picked[:, :half]))
        if level == second_at:
            coeffs, picked_second = lax.optimization_barrier((coeffs, picked[:, half:]))
        partner = from_partner(coeffs, axis, bit)
        coeffs = translate(weights[level], coeffs, partner)
    coeffs = coeffs.reshape(group_total, rank_size, group_width).transpose(1, 0, 2)
    coeffs = coeffs.reshape(rank_size, total_cols)
    coeff_bf = coeffs.astype(jnp.bfloat16).reshape(rank_size, leaf_count, rhs_count)
    far_term = jnp.einsum("lrp,rls->slp", out_basis, coeff_bf, preferred_element_type=jnp.float32)
    own_term = jnp.einsum(
        "lpq,slq->slp", band_blocks[:, 0], leaves, preferred_element_type=jnp.float32
    )
    partner_first = jnp.einsum(
        "lpq,slq->slp", band_blocks[:half, 1], picked_first, preferred_element_type=jnp.float32
    )
    partner_second = jnp.einsum(
        "lpq,slq->slp", band_blocks[half:, 1], picked_second, preferred_element_type=jnp.float32
    )
    partner_term = jnp.concatenate([partner_first, partner_second], axis=1)
    return (far_term + own_term + partner_term).reshape(rhs_count, point_count)


def solution(mesh):
    return jax.shard_map(
        local,
        mesh=mesh,
        in_specs=(
            P(None, ("gx", "gy")),
            P(("gx", "gy")),
            P(("gx", "gy")),
            P(("gx", "gy"), None, None),
            P(("gx", "gy"), None, None, None),
            P(("gx", "gy"), None, None, None, None, None),
            P(("gx", "gy"), None, None),
        ),
        out_specs=P(None, ("gx", "gy")),
        check_vma=False,
    )
```

```python
import jax
import jax.numpy as jnp
from jax import lax
from jax.experimental import pallas as pl
from jax.experimental.pallas import tpu as pltpu
from jax.sharding import PartitionSpec as P

HW = 16


CHUNK = 128


def gather_kernel(idx_ref, x_ref, o_ref, xt_ref):
    count = o_ref.shape[1]

    def spread(c, carry):
        col = pl.multiple_of(c * CHUNK, CHUNK)
        xt_ref[pl.ds(col, CHUNK), :] = x_ref[:, pl.ds(col, CHUNK)].T
        return carry

    lax.fori_loop(0, count // CHUNK, spread, 0)

    def body(c, carry):
        col = pl.multiple_of(c * CHUNK, CHUNK)
        rows = [xt_ref[pl.ds(idx_ref[col + u], 1), :] for u in range(CHUNK)]
        o_ref[:, pl.ds(col, CHUNK)] = jnp.concatenate(rows, axis=0).T.astype(o_ref.dtype)
        return carry

    lax.fori_loop(0, count // CHUNK, body, 0)


def gather_points(points, index):
    width, count = points.shape
    return pl.pallas_call(
        gather_kernel,
        out_shape=jax.ShapeDtypeStruct((width, count), jnp.bfloat16),
        in_specs=[pl.BlockSpec(memory_space=pltpu.SMEM), pl.BlockSpec(memory_space=pltpu.VMEM)],
        out_specs=pl.BlockSpec(memory_space=pltpu.VMEM),
        scratch_shapes=[pltpu.VMEM((count, width), jnp.float32)],
        compiler_params=pltpu.CompilerParams(vmem_limit_bytes=40 * 1024 * 1024),
        cost_estimate=pl.CostEstimate(flops=0, transcendentals=0, bytes_accessed=count * width * 6),
    )(index, points)


def from_partner(x, axis, distance):
    return lax.ppermute(x, axis, [(i, i ^ 1 << distance) for i in range(lax.axis_size(axis))])


def extended(x, sides, width):
    for axis, dim in sides:
        count, length = (lax.axis_size(axis), x.shape[dim])
        up = [(i, (i + 1) % count) for i in range(count - 1)]
        down = [(j, i) for i, j in up]
        last = lax.slice_in_dim(x, length - width, length, axis=dim)
        initial = lax.slice_in_dim(x, 0, width, axis=dim)
        before = lax.ppermute(last, axis, up)
        after = lax.ppermute(initial, axis, down)
        x = jnp.concatenate([before, x, after], axis=dim)
    return x


def block_diagonals(weights):
    levels, groups, terms, rank, _ = weights.shape
    width = groups * rank
    shape = (groups, rank, width)
    target = lax.broadcasted_iota(jnp.int32, shape, 0) * rank + lax.broadcasted_iota(jnp.int32, shape, 1)
    spread = (lax.broadcasted_iota(jnp.int32, shape, 2) == target).astype(weights.dtype)
    return jnp.einsum(
        "lgtab,gbc->ltgac", weights, spread, precision=lax.Precision.HIGHEST, preferred_element_type=jnp.float32
    ).reshape(levels, terms, width, width)


def translate(level_matrices, own_coeffs, other_coeffs):
    first = jnp.dot(
        level_matrices[0],
        own_coeffs,
        precision=lax.Precision.HIGHEST,
        preferred_element_type=jnp.float32,
    )
    second = jnp.dot(
        level_matrices[1],
        other_coeffs,
        precision=lax.Precision.HIGHEST,
        preferred_element_type=jnp.float32,
    )
    return first + second


def local(points_rhs, morton_order, band_offsets, leaf_basis, band_blocks, translations, out_basis):
    rhs_count, point_count = points_rhs.shape
    leaf_count, rank_size, leaf_size = leaf_basis.shape
    group_total = translations.shape[2]
    total_cols = leaf_count * rhs_count
    group_width = total_cols // group_total
    ordered = gather_points(points_rhs, morton_order)
    leaves = ordered.reshape(rhs_count, leaf_count, leaf_size)
    coeffs = jnp.einsum(
        "lrp,slp->rls", leaf_basis, leaves, preferred_element_type=jnp.float32
    ).reshape(rank_size, total_cols)
    weights = block_diagonals(translations[0])
    low_bits = lax.axis_size("gy").bit_length() - 1
    high_bits = lax.axis_size("gx").bit_length() - 1
    levels = [("gy", bit) for bit in range(low_bits)] + [("gx", bit) for bit in range(high_bits)]
    last = len(levels) - 1
    take_at, own_at, first_at, second_at, own_late_at = (min(k, last) for k in (1, 2, 4, 5, 6))
    padded = extended(ordered, ((("gx", "gy"), 1),), HW * leaf_size)
    blocks_all = padded.reshape(rhs_count, leaf_count + 2 * HW, leaf_size)
    block_index = jnp.arange(leaf_count, dtype=jnp.int32) + HW + band_offsets
    half = leaf_count // 2
    coeffs = coeffs.reshape(rank_size, group_total, group_width).transpose(1, 0, 2)
    coeffs = coeffs.reshape(group_total * rank_size, group_width)
    picked = None
    for level, (axis, bit) in enumerate(levels):
        if level == take_at:
            coeffs, blocks_all = lax.optimization_barrier((coeffs, blocks_all))
            picked = jnp.take(blocks_all, block_index, axis=1)
        if level == own_at:
            coeffs, own_first = lax.optimization_barrier((coeffs, leaves[:, :half]))
        if level == own_late_at:
            coeffs, own_second = lax.optimization_barrier((coeffs, leaves[:, half:]))
        if level == first_at:
            coeffs, picked_first = lax.optimization_barrier((coeffs, picked[:, :half]))
        if level == second_at:
            coeffs, picked_second = lax.optimization_barrier((coeffs, picked[:, half:]))
        partner = from_partner(coeffs, axis, bit)
        coeffs = translate(weights[level], coeffs, partner)
    coeffs = coeffs.reshape(group_total, rank_size, group_width).transpose(1, 0, 2)
    coeffs = coeffs.reshape(rank_size, total_cols)
    coeff_bf = coeffs.astype(jnp.bfloat16).reshape(rank_size, leaf_count, rhs_count)
    far_term = jnp.einsum("lrp,rls->slp", out_basis, coeff_bf, preferred_element_type=jnp.float32)
    own_term = jnp.concatenate(
        [
            jnp.einsum("lpq,slq->slp", band_blocks[:half, 0], own_first, preferred_element_type=jnp.float32),
            jnp.einsum("lpq,slq->slp", band_blocks[half:, 0], own_second, preferred_element_type=jnp.float32),
        ],
        axis=1,
    )
    partner_first = jnp.einsum(
        "lpq,slq->slp", band_blocks[:half, 1], picked_first, preferred_element_type=jnp.float32
    )
    partner_second = jnp.einsum(
        "lpq,slq->slp", band_blocks[half:, 1], picked_second, preferred_element_type=jnp.float32
    )
    partner_term = jnp.concatenate([partner_first, partner_second], axis=1)
    return (far_term + own_term + partner_term).reshape(rhs_count, point_count)


def solution(mesh):
    return jax.shard_map(
        local,
        mesh=mesh,
        in_specs=(
            P(None, ("gx", "gy")),
            P(("gx", "gy")),
            P(("gx", "gy")),
            P(("gx", "gy"), None, None),
            P(("gx", "gy"), None, None, None),
            P(("gx", "gy"), None, None, None, None, None),
            P(("gx", "gy"), None, None),
        ),
        out_specs=P(None, ("gx", "gy")),
        check_vma=False,
    )
```

```python
import jax
import jax.numpy as jnp
from jax import lax
from jax.experimental import pallas as pl
from jax.experimental.pallas import tpu as pltpu
from jax.sharding import PartitionSpec as P

HW = 16


CHUNK = 128


def gather_kernel(idx_ref, x_ref, o_ref, xt_ref):
    count = o_ref.shape[1]

    def spread(c, carry):
        col = pl.multiple_of(c * CHUNK, CHUNK)
        xt_ref[pl.ds(col, CHUNK), :] = x_ref[:, pl.ds(col, CHUNK)].T
        return carry

    lax.fori_loop(0, count // CHUNK, spread, 0)

    def body(c, carry):
        col = pl.multiple_of(c * CHUNK, CHUNK)
        rows = [xt_ref[pl.ds(idx_ref[col + u], 1), :] for u in range(CHUNK)]
        o_ref[:, pl.ds(col, CHUNK)] = jnp.concatenate(rows, axis=0).T.astype(o_ref.dtype)
        return carry

    lax.fori_loop(0, count // CHUNK, body, 0)


def gather_points(points, index):
    width, count = points.shape
    return pl.pallas_call(
        gather_kernel,
        out_shape=jax.ShapeDtypeStruct((width, count), jnp.bfloat16),
        in_specs=[pl.BlockSpec(memory_space=pltpu.SMEM), pl.BlockSpec(memory_space=pltpu.VMEM)],
        out_specs=pl.BlockSpec(memory_space=pltpu.VMEM),
        scratch_shapes=[pltpu.VMEM((count, width), jnp.float32)],
        compiler_params=pltpu.CompilerParams(vmem_limit_bytes=40 * 1024 * 1024),
        cost_estimate=pl.CostEstimate(flops=0, transcendentals=0, bytes_accessed=count * width * 6),
    )(index, points)


def from_partner(x, axis, distance):
    return lax.ppermute(x, axis, [(i, i ^ 1 << distance) for i in range(lax.axis_size(axis))])


def extended(x, sides, width):
    for axis, dim in sides:
        count, length = (lax.axis_size(axis), x.shape[dim])
        up = [(i, (i + 1) % count) for i in range(count - 1)]
        down = [(j, i) for i, j in up]
        last = lax.slice_in_dim(x, length - width, length, axis=dim)
        initial = lax.slice_in_dim(x, 0, width, axis=dim)
        before = lax.ppermute(last, axis, up)
        after = lax.ppermute(initial, axis, down)
        x = jnp.concatenate([before, x, after], axis=dim)
    return x


def block_diagonals(weights):
    levels, groups, terms, rank, _ = weights.shape
    width = groups * rank
    shape = (groups, rank, width)
    target = lax.broadcasted_iota(jnp.int32, shape, 0) * rank + lax.broadcasted_iota(jnp.int32, shape, 1)
    spread = (lax.broadcasted_iota(jnp.int32, shape, 2) == target).astype(weights.dtype)
    return jnp.einsum(
        "lgtab,gbc->ltgac", weights, spread, precision=lax.Precision.HIGHEST, preferred_element_type=jnp.float32
    ).reshape(levels, terms, width, width)


def translate(level_matrices, own_coeffs, other_coeffs):
    first = jnp.dot(
        level_matrices[0],
        own_coeffs,
        precision=lax.Precision.HIGH,
        preferred_element_type=jnp.float32,
    )
    second = jnp.dot(
        level_matrices[1],
        other_coeffs,
        precision=lax.Precision.HIGH,
        preferred_element_type=jnp.float32,
    )
    return first + second


def local(points_rhs, morton_order, band_offsets, leaf_basis, band_blocks, translations, out_basis):
    rhs_count, point_count = points_rhs.shape
    leaf_count, rank_size, leaf_size = leaf_basis.shape
    group_total = translations.shape[2]
    total_cols = leaf_count * rhs_count
    group_width = total_cols // group_total
    ordered = gather_points(points_rhs, morton_order)
    leaves = ordered.reshape(rhs_count, leaf_count, leaf_size)
    coeffs = jnp.einsum(
        "lrp,slp->rls", leaf_basis, leaves, preferred_element_type=jnp.float32
    ).reshape(rank_size, total_cols)
    weights = block_diagonals(translations[0])
    low_bits = lax.axis_size("gy").bit_length() - 1
    high_bits = lax.axis_size("gx").bit_length() - 1
    levels = [("gy", bit) for bit in range(low_bits)] + [("gx", bit) for bit in range(high_bits)]
    last = len(levels) - 1
    take_at, own_at, first_at, second_at, own_late_at = (min(k, last) for k in (1, 2, 4, 5, 6))
    padded = extended(ordered, ((("gx", "gy"), 1),), HW * leaf_size)
    blocks_all = padded.reshape(rhs_count, leaf_count + 2 * HW, leaf_size)
    block_index = jnp.arange(leaf_count, dtype=jnp.int32) + HW + band_offsets
    half = leaf_count // 2
    coeffs = coeffs.reshape(rank_size, group_total, group_width).transpose(1, 0, 2)
    coeffs = coeffs.reshape(group_total * rank_size, group_width)
    picked = None
    for level, (axis, bit) in enumerate(levels):
        if level == take_at:
            coeffs, blocks_all = lax.optimization_barrier((coeffs, blocks_all))
            picked = jnp.take(blocks_all, block_index, axis=1)
        if level == own_at:
            coeffs, own_first = lax.optimization_barrier((coeffs, leaves[:, :half]))
        if level == own_late_at:
            coeffs, own_second = lax.optimization_barrier((coeffs, leaves[:, half:]))
        if level == first_at:
            coeffs, picked_first = lax.optimization_barrier((coeffs, picked[:, :half]))
        if level == second_at:
            coeffs, picked_second = lax.optimization_barrier((coeffs, picked[:, half:]))
        partner = from_partner(coeffs, axis, bit)
        coeffs = translate(weights[level], coeffs, partner)
    coeffs = coeffs.reshape(group_total, rank_size, group_width).transpose(1, 0, 2)
    coeffs = coeffs.reshape(rank_size, total_cols)
    coeff_bf = coeffs.astype(jnp.bfloat16).reshape(rank_size, leaf_count, rhs_count)
    far_term = jnp.einsum("lrp,rls->slp", out_basis, coeff_bf, preferred_element_type=jnp.float32)
    own_term = jnp.concatenate(
        [
            jnp.einsum("lpq,slq->slp", band_blocks[:half, 0], own_first, preferred_element_type=jnp.float32),
            jnp.einsum("lpq,slq->slp", band_blocks[half:, 0], own_second, preferred_element_type=jnp.float32),
        ],
        axis=1,
    )
    partner_first = jnp.einsum(
        "lpq,slq->slp", band_blocks[:half, 1], picked_first, preferred_element_type=jnp.float32
    )
    partner_second = jnp.einsum(
        "lpq,slq->slp", band_blocks[half:, 1], picked_second, preferred_element_type=jnp.float32
    )
    partner_term = jnp.concatenate([partner_first, partner_second], axis=1)
    return (far_term + own_term + partner_term).reshape(rhs_count, point_count)


def solution(mesh):
    return jax.shard_map(
        local,
        mesh=mesh,
        in_specs=(
            P(None, ("gx", "gy")),
            P(("gx", "gy")),
            P(("gx", "gy")),
            P(("gx", "gy"), None, None),
            P(("gx", "gy"), None, None, None),
            P(("gx", "gy"), None, None, None, None, None),
            P(("gx", "gy"), None, None),
        ),
        out_specs=P(None, ("gx", "gy")),
        check_vma=False,
    )
```

```python
import jax
import jax.numpy as jnp
from jax import lax
from jax.experimental import pallas as pl
from jax.experimental.pallas import tpu as pltpu
from jax.sharding import PartitionSpec as P

HW = 16


CHUNK = 128
PARTS = 4


def gather_kernel(idx_ref, x_hbm, o_ref, x_ref, xt_ref, sems):
    count = o_ref.shape[1]
    span = count // PARTS
    fetches = [
        pltpu.make_async_copy(x_hbm.at[:, pl.ds(q * span, span)], x_ref.at[:, pl.ds(q * span, span)], sems.at[q])
        for q in range(PARTS)
    ]
    for fetch in fetches:
        fetch.start()
    for q, fetch in enumerate(fetches):
        fetch.wait()

        def spread(c, carry, q=q):
            col = pl.multiple_of(q * span + c * CHUNK, CHUNK)
            xt_ref[pl.ds(col, CHUNK), :] = x_ref[:, pl.ds(col, CHUNK)].T
            return carry

        lax.fori_loop(0, span // CHUNK, spread, 0)

    def body(c, carry):
        col = pl.multiple_of(c * CHUNK, CHUNK)
        rows = [xt_ref[pl.ds(idx_ref[col + u], 1), :] for u in range(CHUNK)]
        o_ref[:, pl.ds(col, CHUNK)] = jnp.concatenate(rows, axis=0).T.astype(o_ref.dtype)
        return carry

    lax.fori_loop(0, count // CHUNK, body, 0)


def gather_points(points, index):
    width, count = points.shape
    return pl.pallas_call(
        gather_kernel,
        out_shape=jax.ShapeDtypeStruct((width, count), jnp.bfloat16),
        in_specs=[pl.BlockSpec(memory_space=pltpu.SMEM), pl.BlockSpec(memory_space=pl.ANY)],
        out_specs=pl.BlockSpec(memory_space=pltpu.VMEM),
        scratch_shapes=[
            pltpu.VMEM((width, count), jnp.float32),
            pltpu.VMEM((count, width), jnp.float32),
            pltpu.SemaphoreType.DMA((PARTS,)),
        ],
        compiler_params=pltpu.CompilerParams(vmem_limit_bytes=67043328),
        cost_estimate=pl.CostEstimate(flops=0, transcendentals=0, bytes_accessed=count * width * 6),
    )(index, points)


def from_partner(x, axis, distance):
    return lax.ppermute(x, axis, [(i, i ^ 1 << distance) for i in range(lax.axis_size(axis))])


def extended(x, sides, width):
    for axis, dim in sides:
        count, length = (lax.axis_size(axis), x.shape[dim])
        up = [(i, (i + 1) % count) for i in range(count - 1)]
        down = [(j, i) for i, j in up]
        last = lax.slice_in_dim(x, length - width, length, axis=dim)
        initial = lax.slice_in_dim(x, 0, width, axis=dim)
        before = lax.ppermute(last, axis, up)
        after = lax.ppermute(initial, axis, down)
        x = jnp.concatenate([before, x, after], axis=dim)
    return x


def block_diagonals(weights):
    levels, groups, terms, rank, _ = weights.shape
    width = groups * rank
    shape = (groups, rank, width)
    target = lax.broadcasted_iota(jnp.int32, shape, 0) * rank + lax.broadcasted_iota(jnp.int32, shape, 1)
    spread = (lax.broadcasted_iota(jnp.int32, shape, 2) == target).astype(weights.dtype)
    return jnp.einsum(
        "lgtab,gbc->ltgac", weights, spread, precision=lax.Precision.HIGHEST, preferred_element_type=jnp.float32
    ).reshape(levels, terms, width, width)


def translate(level_matrices, own_coeffs, other_coeffs):
    first = jnp.dot(
        level_matrices[0],
        own_coeffs,
        precision=lax.Precision.HIGH,
        preferred_element_type=jnp.float32,
    )
    second = jnp.dot(
        level_matrices[1],
        other_coeffs,
        precision=lax.Precision.HIGH,
        preferred_element_type=jnp.float32,
    )
    return first + second


def local(points_rhs, morton_order, band_offsets, leaf_basis, band_blocks, translations, out_basis):
    rhs_count, point_count = points_rhs.shape
    leaf_count, rank_size, leaf_size = leaf_basis.shape
    group_total = translations.shape[2]
    total_cols = leaf_count * rhs_count
    group_width = total_cols // group_total
    ordered = gather_points(points_rhs, morton_order)
    leaves = ordered.reshape(rhs_count, leaf_count, leaf_size)
    coeffs = jnp.einsum(
        "lrp,slp->rls", leaf_basis, leaves, preferred_element_type=jnp.float32
    ).reshape(rank_size, total_cols)
    weights = block_diagonals(translations[0])
    low_bits = lax.axis_size("gy").bit_length() - 1
    high_bits = lax.axis_size("gx").bit_length() - 1
    levels = [("gy", bit) for bit in range(low_bits)] + [("gx", bit) for bit in range(high_bits)]
    last = len(levels) - 1
    take_at, own_at, first_at, second_at, own_late_at = (min(k, last) for k in (1, 2, 4, 5, 6))
    padded = extended(ordered, ((("gx", "gy"), 1),), HW * leaf_size)
    blocks_all = padded.reshape(rhs_count, leaf_count + 2 * HW, leaf_size)
    block_index = jnp.arange(leaf_count, dtype=jnp.int32) + HW + band_offsets
    half = leaf_count // 2
    coeffs = coeffs.reshape(rank_size, group_total, group_width).transpose(1, 0, 2)
    coeffs = coeffs.reshape(group_total * rank_size, group_width)
    picked = None
    for level, (axis, bit) in enumerate(levels):
        if level == take_at:
            coeffs, blocks_all = lax.optimization_barrier((coeffs, blocks_all))
            picked = jnp.take(blocks_all, block_index, axis=1)
        if level == own_at:
            coeffs, own_first = lax.optimization_barrier((coeffs, leaves[:, :half]))
        if level == own_late_at:
            coeffs, own_second = lax.optimization_barrier((coeffs, leaves[:, half:]))
        if level == first_at:
            coeffs, picked_first = lax.optimization_barrier((coeffs, picked[:, :half]))
        if level == second_at:
            coeffs, picked_second = lax.optimization_barrier((coeffs, picked[:, half:]))
        partner = from_partner(coeffs, axis, bit)
        coeffs = translate(weights[level], coeffs, partner)
    coeffs = coeffs.reshape(group_total, rank_size, group_width).transpose(1, 0, 2)
    coeffs = coeffs.reshape(rank_size, total_cols)
    coeff_bf = coeffs.astype(jnp.bfloat16).reshape(rank_size, leaf_count, rhs_count)
    far_term = jnp.einsum("lrp,rls->slp", out_basis, coeff_bf, preferred_element_type=jnp.float32)
    own_term = jnp.concatenate(
        [
            jnp.einsum("lpq,slq->slp", band_blocks[:half, 0], own_first, preferred_element_type=jnp.float32),
            jnp.einsum("lpq,slq->slp", band_blocks[half:, 0], own_second, preferred_element_type=jnp.float32),
        ],
        axis=1,
    )
    partner_first = jnp.einsum(
        "lpq,slq->slp", band_blocks[:half, 1], picked_first, preferred_element_type=jnp.float32
    )
    partner_second = jnp.einsum(
        "lpq,slq->slp", band_blocks[half:, 1], picked_second, preferred_element_type=jnp.float32
    )
    partner_term = jnp.concatenate([partner_first, partner_second], axis=1)
    return (far_term + own_term + partner_term).reshape(rhs_count, point_count)


def solution(mesh):
    return jax.shard_map(
        local,
        mesh=mesh,
        in_specs=(
            P(None, ("gx", "gy")),
            P(("gx", "gy")),
            P(("gx", "gy")),
            P(("gx", "gy"), None, None),
            P(("gx", "gy"), None, None, None),
            P(("gx", "gy"), None, None, None, None, None),
            P(("gx", "gy"), None, None),
        ),
        out_specs=P(None, ("gx", "gy")),
        check_vma=False,
    )
```

```python
import jax
import jax.numpy as jnp
from jax import lax
from jax.experimental import pallas as pl
from jax.experimental.pallas import tpu as pltpu
from jax.sharding import PartitionSpec as P

HW = 16


CHUNK = 128
PARTS = 4


def gather_kernel(idx_ref, x_hbm, o_ref, x_ref, xt_ref, sems):
    count = o_ref.shape[1]
    span = count // PARTS
    fetches = [
        pltpu.make_async_copy(x_hbm.at[:, pl.ds(q * span, span)], x_ref.at[:, pl.ds(q * span, span)], sems.at[q])
        for q in range(PARTS)
    ]
    for fetch in fetches:
        fetch.start()
    for q, fetch in enumerate(fetches):
        fetch.wait()

        def spread(c, carry, q=q):
            col = pl.multiple_of(q * span + c * CHUNK, CHUNK)
            xt_ref[pl.ds(col, CHUNK), :] = x_ref[:, pl.ds(col, CHUNK)].T
            return carry

        lax.fori_loop(0, span // CHUNK, spread, 0)

    def body(c, carry):
        col = pl.multiple_of(c * CHUNK, CHUNK)
        rows = [xt_ref[pl.ds(idx_ref[col + u], 1), :] for u in range(CHUNK)]
        o_ref[:, pl.ds(col, CHUNK)] = jnp.concatenate(rows, axis=0).T.astype(o_ref.dtype)
        return carry

    lax.fori_loop(0, count // CHUNK, body, 0)


def gather_points(points, index):
    width, count = points.shape
    return pl.pallas_call(
        gather_kernel,
        out_shape=jax.ShapeDtypeStruct((width, count), jnp.bfloat16),
        in_specs=[pl.BlockSpec(memory_space=pltpu.SMEM), pl.BlockSpec(memory_space=pl.ANY)],
        out_specs=pl.BlockSpec(memory_space=pltpu.VMEM),
        scratch_shapes=[
            pltpu.VMEM((width, count), jnp.float32),
            pltpu.VMEM((count, width), jnp.float32),
            pltpu.SemaphoreType.DMA((PARTS,)),
        ],
        compiler_params=pltpu.CompilerParams(vmem_limit_bytes=67043328),
        cost_estimate=pl.CostEstimate(flops=0, transcendentals=0, bytes_accessed=count * width * 6),
    )(index, points)


def from_partner(x, axis, distance):
    return lax.ppermute(x, axis, [(i, i ^ 1 << distance) for i in range(lax.axis_size(axis))])


def extended(x, sides, width):
    for axis, dim in sides:
        count, length = (lax.axis_size(axis), x.shape[dim])
        up = [(i, (i + 1) % count) for i in range(count - 1)]
        down = [(j, i) for i, j in up]
        last = lax.slice_in_dim(x, length - width, length, axis=dim)
        initial = lax.slice_in_dim(x, 0, width, axis=dim)
        before = lax.ppermute(last, axis, up)
        after = lax.ppermute(initial, axis, down)
        x = jnp.concatenate([before, x, after], axis=dim)
    return x


def block_diagonals(weights):
    levels, groups, terms, rank, _ = weights.shape
    width = groups * rank
    shape = (groups, rank, width)
    target = lax.broadcasted_iota(jnp.int32, shape, 1) * groups + lax.broadcasted_iota(jnp.int32, shape, 0)
    spread = (lax.broadcasted_iota(jnp.int32, shape, 2) == target).astype(weights.dtype)
    return jnp.einsum(
        "lgtab,gbc->ltagc", weights, spread, precision=lax.Precision.HIGHEST, preferred_element_type=jnp.float32
    ).reshape(levels, terms, width, width)


def translate(level_matrices, own_coeffs, other_coeffs):
    first = jnp.dot(
        level_matrices[0],
        own_coeffs,
        precision=lax.Precision.HIGH,
        preferred_element_type=jnp.float32,
    )
    second = jnp.dot(
        level_matrices[1],
        other_coeffs,
        precision=lax.Precision.HIGH,
        preferred_element_type=jnp.float32,
    )
    return first + second


def local(points_rhs, morton_order, band_offsets, leaf_basis, band_blocks, translations, out_basis):
    rhs_count, point_count = points_rhs.shape
    leaf_count, rank_size, leaf_size = leaf_basis.shape
    group_total = translations.shape[2]
    total_cols = leaf_count * rhs_count
    group_width = total_cols // group_total
    ordered = gather_points(points_rhs, morton_order)
    leaves = ordered.reshape(rhs_count, leaf_count, leaf_size)
    coeffs = jnp.einsum(
        "lrp,slp->rls", leaf_basis, leaves, preferred_element_type=jnp.float32
    ).reshape(rank_size, total_cols)
    weights = block_diagonals(translations[0])
    low_bits = lax.axis_size("gy").bit_length() - 1
    high_bits = lax.axis_size("gx").bit_length() - 1
    levels = [("gy", bit) for bit in range(low_bits)] + [("gx", bit) for bit in range(high_bits)]
    last = len(levels) - 1
    take_at, own_at, first_at, second_at, own_late_at = (min(k, last) for k in (1, 2, 4, 5, 6))
    padded = extended(ordered, ((("gx", "gy"), 1),), HW * leaf_size)
    blocks_all = padded.reshape(rhs_count, leaf_count + 2 * HW, leaf_size)
    block_index = jnp.arange(leaf_count, dtype=jnp.int32) + HW + band_offsets
    half = leaf_count // 2
    coeffs = coeffs.reshape(rank_size * group_total, group_width)
    picked = None
    for level, (axis, bit) in enumerate(levels):
        if level == take_at:
            coeffs, blocks_all = lax.optimization_barrier((coeffs, blocks_all))
            picked = jnp.take(blocks_all, block_index, axis=1)
        if level == own_at:
            coeffs, own_first = lax.optimization_barrier((coeffs, leaves[:, :half]))
        if level == own_late_at:
            coeffs, own_second = lax.optimization_barrier((coeffs, leaves[:, half:]))
        if level == first_at:
            coeffs, picked_first = lax.optimization_barrier((coeffs, picked[:, :half]))
        if level == second_at:
            coeffs, picked_second = lax.optimization_barrier((coeffs, picked[:, half:]))
        partner = from_partner(coeffs, axis, bit)
        coeffs = translate(weights[level], coeffs, partner)
    coeffs = coeffs.reshape(rank_size, total_cols)
    coeff_bf = coeffs.astype(jnp.bfloat16).reshape(rank_size, leaf_count, rhs_count)
    far_term = jnp.einsum("lrp,rls->slp", out_basis, coeff_bf, preferred_element_type=jnp.float32)
    own_term = jnp.concatenate(
        [
            jnp.einsum("lpq,slq->slp", band_blocks[:half, 0], own_first, preferred_element_type=jnp.float32),
            jnp.einsum("lpq,slq->slp", band_blocks[half:, 0], own_second, preferred_element_type=jnp.float32),
        ],
        axis=1,
    )
    partner_first = jnp.einsum(
        "lpq,slq->slp", band_blocks[:half, 1], picked_first, preferred_element_type=jnp.float32
    )
    partner_second = jnp.einsum(
        "lpq,slq->slp", band_blocks[half:, 1], picked_second, preferred_element_type=jnp.float32
    )
    partner_term = jnp.concatenate([partner_first, partner_second], axis=1)
    return (far_term + own_term + partner_term).reshape(rhs_count, point_count)


def solution(mesh):
    return jax.shard_map(
        local,
        mesh=mesh,
        in_specs=(
            P(None, ("gx", "gy")),
            P(("gx", "gy")),
            P(("gx", "gy")),
            P(("gx", "gy"), None, None),
            P(("gx", "gy"), None, None, None),
            P(("gx", "gy"), None, None, None, None, None),
            P(("gx", "gy"), None, None),
        ),
        out_specs=P(None, ("gx", "gy")),
        check_vma=False,
    )
```

```python
import jax
import jax.numpy as jnp
from jax import lax
from jax.experimental import pallas as pl
from jax.experimental.pallas import tpu as pltpu
from jax.sharding import PartitionSpec as P

HW = 16


CHUNK = 128
PARTS = 4


def gather_kernel(idx_ref, x_hbm, o_ref, x_ref, xt_ref, sems):
    count = o_ref.shape[1]
    span = count // PARTS
    fetches = [
        pltpu.make_async_copy(x_hbm.at[:, pl.ds(q * span, span)], x_ref.at[:, pl.ds(q * span, span)], sems.at[q])
        for q in range(PARTS)
    ]
    for fetch in fetches:
        fetch.start()
    for q, fetch in enumerate(fetches):
        fetch.wait()

        def spread(c, carry, q=q):
            col = pl.multiple_of(q * span + c * CHUNK, CHUNK)
            xt_ref[pl.ds(col, CHUNK), :] = x_ref[:, pl.ds(col, CHUNK)].T
            return carry

        lax.fori_loop(0, span // CHUNK, spread, 0)

    def body(c, carry):
        col = pl.multiple_of(c * CHUNK, CHUNK)
        rows = [xt_ref[pl.ds(idx_ref[col + u], 1), :] for u in range(CHUNK)]
        o_ref[:, pl.ds(col, CHUNK)] = jnp.concatenate(rows, axis=0).T.astype(o_ref.dtype)
        return carry

    lax.fori_loop(0, count // CHUNK, body, 0, unroll=2)


def gather_points(points, index):
    width, count = points.shape
    return pl.pallas_call(
        gather_kernel,
        out_shape=jax.ShapeDtypeStruct((width, count), jnp.bfloat16),
        in_specs=[pl.BlockSpec(memory_space=pltpu.SMEM), pl.BlockSpec(memory_space=pl.ANY)],
        out_specs=pl.BlockSpec(memory_space=pltpu.VMEM),
        scratch_shapes=[
            pltpu.VMEM((width, count), jnp.float32),
            pltpu.VMEM((count, width), jnp.float32),
            pltpu.SemaphoreType.DMA((PARTS,)),
        ],
        compiler_params=pltpu.CompilerParams(vmem_limit_bytes=67043328),
        cost_estimate=pl.CostEstimate(flops=0, transcendentals=0, bytes_accessed=count * width * 6),
    )(index, points)


def from_partner(x, axis, distance):
    return lax.ppermute(x, axis, [(i, i ^ 1 << distance) for i in range(lax.axis_size(axis))])


def extended(x, sides, width):
    for axis, dim in sides:
        count, length = (lax.axis_size(axis), x.shape[dim])
        up = [(i, (i + 1) % count) for i in range(count - 1)]
        down = [(j, i) for i, j in up]
        last = lax.slice_in_dim(x, length - width, length, axis=dim)
        initial = lax.slice_in_dim(x, 0, width, axis=dim)
        before = lax.ppermute(last, axis, up)
        after = lax.ppermute(initial, axis, down)
        x = jnp.concatenate([before, x, after], axis=dim)
    return x


def block_diagonals(weights):
    levels, groups, terms, rank, _ = weights.shape
    width = groups * rank
    shape = (groups, rank, width)
    target = lax.broadcasted_iota(jnp.int32, shape, 0) * rank + lax.broadcasted_iota(jnp.int32, shape, 1)
    spread = (lax.broadcasted_iota(jnp.int32, shape, 2) == target).astype(weights.dtype)
    return jnp.einsum(
        "lgtab,gbc->ltgac", weights, spread, precision=lax.Precision.HIGHEST, preferred_element_type=jnp.float32
    ).reshape(levels, terms, width, width)


def translate(level_matrices, own_coeffs, other_coeffs):
    first = jnp.dot(
        level_matrices[0],
        own_coeffs,
        precision=lax.Precision.HIGH,
        preferred_element_type=jnp.float32,
    )
    second = jnp.dot(
        level_matrices[1],
        other_coeffs,
        precision=lax.Precision.HIGH,
        preferred_element_type=jnp.float32,
    )
    return first + second


def local(points_rhs, morton_order, band_offsets, leaf_basis, band_blocks, translations, out_basis):
    rhs_count, point_count = points_rhs.shape
    leaf_count, rank_size, leaf_size = leaf_basis.shape
    group_total = translations.shape[2]
    total_cols = leaf_count * rhs_count
    group_width = total_cols // group_total
    ordered = gather_points(points_rhs, morton_order)
    leaves = ordered.reshape(rhs_count, leaf_count, leaf_size)
    coeffs = jnp.einsum(
        "lrp,slp->rls", leaf_basis, leaves, preferred_element_type=jnp.float32
    ).reshape(rank_size, total_cols)
    weights = block_diagonals(translations[0])
    low_bits = lax.axis_size("gy").bit_length() - 1
    high_bits = lax.axis_size("gx").bit_length() - 1
    levels = [("gy", bit) for bit in range(low_bits)] + [("gx", bit) for bit in range(high_bits)]
    last = len(levels) - 1
    take_at, own_at, first_at, second_at, own_late_at = (min(k, last) for k in (1, 2, 4, 5, 6))
    padded = extended(ordered, ((("gx", "gy"), 1),), HW * leaf_size)
    blocks_all = padded.reshape(rhs_count, leaf_count + 2 * HW, leaf_size)
    block_index = jnp.arange(leaf_count, dtype=jnp.int32) + HW + band_offsets
    half = leaf_count // 2
    coeffs = coeffs.reshape(rank_size, group_total, group_width).transpose(1, 0, 2)
    coeffs = coeffs.reshape(group_total * rank_size, group_width)
    picked = None
    for level, (axis, bit) in enumerate(levels):
        if level == take_at:
            coeffs, blocks_all = lax.optimization_barrier((coeffs, blocks_all))
            picked = jnp.take(blocks_all, block_index, axis=1)
        if level == own_at:
            coeffs, own_first = lax.optimization_barrier((coeffs, leaves[:, :half]))
        if level == own_late_at:
            coeffs, own_second = lax.optimization_barrier((coeffs, leaves[:, half:]))
        if level == first_at:
            coeffs, picked_first = lax.optimization_barrier((coeffs, picked[:, :half]))
        if level == second_at:
            coeffs, picked_second = lax.optimization_barrier((coeffs, picked[:, half:]))
        partner = from_partner(coeffs, axis, bit)
        coeffs = translate(weights[level], coeffs, partner)
    coeffs = coeffs.reshape(group_total, rank_size, group_width).transpose(1, 0, 2)
    coeffs = coeffs.reshape(rank_size, total_cols)
    coeff_bf = coeffs.astype(jnp.bfloat16).reshape(rank_size, leaf_count, rhs_count)
    far_term = jnp.einsum("lrp,rls->slp", out_basis, coeff_bf, preferred_element_type=jnp.float32)
    own_term = jnp.concatenate(
        [
            jnp.einsum("lpq,slq->slp", band_blocks[:half, 0], own_first, preferred_element_type=jnp.float32),
            jnp.einsum("lpq,slq->slp", band_blocks[half:, 0], own_second, preferred_element_type=jnp.float32),
        ],
        axis=1,
    )
    partner_first = jnp.einsum(
        "lpq,slq->slp", band_blocks[:half, 1], picked_first, preferred_element_type=jnp.float32
    )
    partner_second = jnp.einsum(
        "lpq,slq->slp", band_blocks[half:, 1], picked_second, preferred_element_type=jnp.float32
    )
    partner_term = jnp.concatenate([partner_first, partner_second], axis=1)
    return (far_term + own_term + partner_term).reshape(rhs_count, point_count)


def solution(mesh):
    return jax.shard_map(
        local,
        mesh=mesh,
        in_specs=(
            P(None, ("gx", "gy")),
            P(("gx", "gy")),
            P(("gx", "gy")),
            P(("gx", "gy"), None, None),
            P(("gx", "gy"), None, None, None),
            P(("gx", "gy"), None, None, None, None, None),
            P(("gx", "gy"), None, None),
        ),
        out_specs=P(None, ("gx", "gy")),
        check_vma=False,
    )
```

```python
import jax
import jax.numpy as jnp
from jax import lax
from jax.experimental import pallas as pl
from jax.experimental.pallas import tpu as pltpu
from jax.sharding import PartitionSpec as P

HW = 16


CHUNK = 128
PARTS = 4


def gather_kernel(idx_ref, x_hbm, o_ref, x_ref, xt_ref, sems):
    count = o_ref.shape[1]
    span = count // PARTS
    fetches = [
        pltpu.make_async_copy(x_hbm.at[:, pl.ds(q * span, span)], x_ref.at[:, pl.ds(q * span, span)], sems.at[q])
        for q in range(PARTS)
    ]
    for fetch in fetches:
        fetch.start()
    for q, fetch in enumerate(fetches):
        fetch.wait()

        def spread(c, carry, q=q):
            col = pl.multiple_of(q * span + c * CHUNK, CHUNK)
            xt_ref[pl.ds(col, CHUNK), :] = x_ref[:, pl.ds(col, CHUNK)].T
            return carry

        lax.fori_loop(0, span // CHUNK, spread, 0, unroll=2)

    def body(c, carry):
        col = pl.multiple_of(c * CHUNK, CHUNK)
        rows = [xt_ref[pl.ds(idx_ref[col + u], 1), :] for u in range(CHUNK)]
        o_ref[:, pl.ds(col, CHUNK)] = jnp.concatenate(rows, axis=0).T.astype(o_ref.dtype)
        return carry

    lax.fori_loop(0, count // CHUNK, body, 0, unroll=4)


def gather_points(points, index):
    width, count = points.shape
    return pl.pallas_call(
        gather_kernel,
        out_shape=jax.ShapeDtypeStruct((width, count), jnp.bfloat16),
        in_specs=[pl.BlockSpec(memory_space=pltpu.SMEM), pl.BlockSpec(memory_space=pl.ANY)],
        out_specs=pl.BlockSpec(memory_space=pltpu.VMEM),
        scratch_shapes=[
            pltpu.VMEM((width, count), jnp.float32),
            pltpu.VMEM((count, width), jnp.float32),
            pltpu.SemaphoreType.DMA((PARTS,)),
        ],
        compiler_params=pltpu.CompilerParams(vmem_limit_bytes=67043328),
        cost_estimate=pl.CostEstimate(flops=0, transcendentals=0, bytes_accessed=count * width * 6),
    )(index, points)


def from_partner(x, axis, distance):
    return lax.ppermute(x, axis, [(i, i ^ 1 << distance) for i in range(lax.axis_size(axis))])


def extended(x, sides, width):
    for axis, dim in sides:
        count, length = (lax.axis_size(axis), x.shape[dim])
        up = [(i, (i + 1) % count) for i in range(count - 1)]
        down = [(j, i) for i, j in up]
        last = lax.slice_in_dim(x, length - width, length, axis=dim)
        initial = lax.slice_in_dim(x, 0, width, axis=dim)
        before = lax.ppermute(last, axis, up)
        after = lax.ppermute(initial, axis, down)
        x = jnp.concatenate([before, x, after], axis=dim)
    return x


def block_diagonals(weights):
    levels, groups, terms, rank, _ = weights.shape
    width = groups * rank
    shape = (groups, rank, width)
    target = lax.broadcasted_iota(jnp.int32, shape, 0) * rank + lax.broadcasted_iota(jnp.int32, shape, 1)
    spread = (lax.broadcasted_iota(jnp.int32, shape, 2) == target).astype(weights.dtype)
    return jnp.einsum(
        "lgtab,gbc->ltgac", weights, spread, precision=lax.Precision.HIGHEST, preferred_element_type=jnp.float32
    ).reshape(levels, terms, width, width)


def translate(level_matrices, own_coeffs, other_coeffs):
    first = jnp.dot(
        level_matrices[0],
        own_coeffs,
        precision=lax.Precision.HIGH,
        preferred_element_type=jnp.float32,
    )
    second = jnp.dot(
        level_matrices[1],
        other_coeffs,
        precision=lax.Precision.HIGH,
        preferred_element_type=jnp.float32,
    )
    return first + second


def local(points_rhs, morton_order, band_offsets, leaf_basis, band_blocks, translations, out_basis):
    rhs_count, point_count = points_rhs.shape
    leaf_count, rank_size, leaf_size = leaf_basis.shape
    group_total = translations.shape[2]
    total_cols = leaf_count * rhs_count
    group_width = total_cols // group_total
    ordered = gather_points(points_rhs, morton_order)
    leaves = ordered.reshape(rhs_count, leaf_count, leaf_size)
    coeffs = jnp.einsum(
        "lrp,slp->rls", leaf_basis, leaves, preferred_element_type=jnp.float32
    ).reshape(rank_size, total_cols)
    weights = block_diagonals(translations[0])
    low_bits = lax.axis_size("gy").bit_length() - 1
    high_bits = lax.axis_size("gx").bit_length() - 1
    levels = [("gy", bit) for bit in range(low_bits)] + [("gx", bit) for bit in range(high_bits)]
    last = len(levels) - 1
    take_at, own_at, first_at, second_at, own_late_at = (min(k, last) for k in (1, 2, 4, 5, 6))
    padded = extended(ordered, ((("gx", "gy"), 1),), HW * leaf_size)
    blocks_all = padded.reshape(rhs_count, leaf_count + 2 * HW, leaf_size)
    block_index = jnp.arange(leaf_count, dtype=jnp.int32) + HW + band_offsets
    half = leaf_count // 2
    coeffs = coeffs.reshape(rank_size, group_total, group_width).transpose(1, 0, 2)
    coeffs = coeffs.reshape(group_total * rank_size, group_width)
    picked = None
    for level, (axis, bit) in enumerate(levels):
        if level == take_at:
            coeffs, blocks_all = lax.optimization_barrier((coeffs, blocks_all))
            picked = jnp.take(blocks_all, block_index, axis=1)
        if level == own_at:
            coeffs, own_first = lax.optimization_barrier((coeffs, leaves[:, :half]))
        if level == own_late_at:
            coeffs, own_second = lax.optimization_barrier((coeffs, leaves[:, half:]))
        if level == first_at:
            coeffs, picked_first = lax.optimization_barrier((coeffs, picked[:, :half]))
        if level == second_at:
            coeffs, picked_second = lax.optimization_barrier((coeffs, picked[:, half:]))
        partner = from_partner(coeffs, axis, bit)
        coeffs = translate(weights[level], coeffs, partner)
    coeffs = coeffs.reshape(group_total, rank_size, group_width).transpose(1, 0, 2)
    coeffs = coeffs.reshape(rank_size, total_cols)
    coeff_bf = coeffs.astype(jnp.bfloat16).reshape(rank_size, leaf_count, rhs_count)
    far_term = jnp.einsum("lrp,rls->slp", out_basis, coeff_bf, preferred_element_type=jnp.float32)
    own_term = jnp.concatenate(
        [
            jnp.einsum("lpq,slq->slp", band_blocks[:half, 0], own_first, preferred_element_type=jnp.float32),
            jnp.einsum("lpq,slq->slp", band_blocks[half:, 0], own_second, preferred_element_type=jnp.float32),
        ],
        axis=1,
    )
    partner_first = jnp.einsum(
        "lpq,slq->slp", band_blocks[:half, 1], picked_first, preferred_element_type=jnp.float32
    )
    partner_second = jnp.einsum(
        "lpq,slq->slp", band_blocks[half:, 1], picked_second, preferred_element_type=jnp.float32
    )
    partner_term = jnp.concatenate([partner_first, partner_second], axis=1)
    return (far_term + own_term + partner_term).reshape(rhs_count, point_count)


def solution(mesh):
    return jax.shard_map(
        local,
        mesh=mesh,
        in_specs=(
            P(None, ("gx", "gy")),
            P(("gx", "gy")),
            P(("gx", "gy")),
            P(("gx", "gy"), None, None),
            P(("gx", "gy"), None, None, None),
            P(("gx", "gy"), None, None, None, None, None),
            P(("gx", "gy"), None, None),
        ),
        out_specs=P(None, ("gx", "gy")),
        check_vma=False,
    )
```

```python
import jax
import jax.numpy as jnp
from jax import lax
from jax.experimental import pallas as pl
from jax.experimental.pallas import tpu as pltpu
from jax.sharding import PartitionSpec as P

HW = 16


CHUNK = 128
PARTS = 4


def gather_kernel(idx_ref, x_hbm, o_ref, x_ref, xt_ref, sems):
    count = o_ref.shape[1]
    span = count // PARTS
    fetches = [
        pltpu.make_async_copy(x_hbm.at[:, pl.ds(q * span, span)], x_ref.at[:, pl.ds(q * span, span)], sems.at[q])
        for q in range(PARTS)
    ]
    for fetch in fetches:
        fetch.start()
    for q, fetch in enumerate(fetches):
        fetch.wait()

        def spread(c, carry, q=q):
            col = pl.multiple_of(q * span + c * CHUNK, CHUNK)
            xt_ref[pl.ds(col, CHUNK), :] = x_ref[:, pl.ds(col, CHUNK)].T
            return carry

        lax.fori_loop(0, span // CHUNK, spread, 0, unroll=4)

    def body(c, carry):
        col = pl.multiple_of(c * CHUNK, CHUNK)
        rows = [xt_ref[pl.ds(idx_ref[col + u], 1), :] for u in range(CHUNK)]
        o_ref[:, pl.ds(col, CHUNK)] = jnp.concatenate(rows, axis=0).T.astype(o_ref.dtype)
        return carry

    lax.fori_loop(0, count // CHUNK, body, 0, unroll=8)


def gather_points(points, index):
    width, count = points.shape
    return pl.pallas_call(
        gather_kernel,
        out_shape=jax.ShapeDtypeStruct((width, count), jnp.bfloat16),
        in_specs=[pl.BlockSpec(memory_space=pltpu.SMEM), pl.BlockSpec(memory_space=pl.ANY)],
        out_specs=pl.BlockSpec(memory_space=pltpu.VMEM),
        scratch_shapes=[
            pltpu.VMEM((width, count), jnp.float32),
            pltpu.VMEM((count, width), jnp.float32),
            pltpu.SemaphoreType.DMA((PARTS,)),
        ],
        compiler_params=pltpu.CompilerParams(vmem_limit_bytes=67043328),
        cost_estimate=pl.CostEstimate(flops=0, transcendentals=0, bytes_accessed=count * width * 6),
    )(index, points)


def from_partner(x, axis, distance):
    return lax.ppermute(x, axis, [(i, i ^ 1 << distance) for i in range(lax.axis_size(axis))])


def extended(x, sides, width):
    for axis, dim in sides:
        count, length = (lax.axis_size(axis), x.shape[dim])
        up = [(i, (i + 1) % count) for i in range(count - 1)]
        down = [(j, i) for i, j in up]
        last = lax.slice_in_dim(x, length - width, length, axis=dim)
        initial = lax.slice_in_dim(x, 0, width, axis=dim)
        before = lax.ppermute(last, axis, up)
        after = lax.ppermute(initial, axis, down)
        x = jnp.concatenate([before, x, after], axis=dim)
    return x


def block_diagonals(weights):
    levels, groups, terms, rank, _ = weights.shape
    width = groups * rank
    shape = (groups, rank, width)
    target = lax.broadcasted_iota(jnp.int32, shape, 0) * rank + lax.broadcasted_iota(jnp.int32, shape, 1)
    spread = (lax.broadcasted_iota(jnp.int32, shape, 2) == target).astype(weights.dtype)
    return jnp.einsum(
        "lgtab,gbc->ltgac", weights, spread, precision=lax.Precision.HIGHEST, preferred_element_type=jnp.float32
    ).reshape(levels, terms, width, width)


def translate(level_matrices, own_coeffs, other_coeffs):
    first = jnp.dot(
        level_matrices[0],
        own_coeffs,
        precision=lax.Precision.HIGH,
        preferred_element_type=jnp.float32,
    )
    second = jnp.dot(
        level_matrices[1],
        other_coeffs,
        precision=lax.Precision.HIGH,
        preferred_element_type=jnp.float32,
    )
    return first + second


def local(points_rhs, morton_order, band_offsets, leaf_basis, band_blocks, translations, out_basis):
    rhs_count, point_count = points_rhs.shape
    leaf_count, rank_size, leaf_size = leaf_basis.shape
    group_total = translations.shape[2]
    total_cols = leaf_count * rhs_count
    group_width = total_cols // group_total
    ordered = gather_points(points_rhs, morton_order)
    leaves = ordered.reshape(rhs_count, leaf_count, leaf_size)
    coeffs = jnp.einsum(
        "lrp,slp->rls", leaf_basis, leaves, preferred_element_type=jnp.float32
    ).reshape(rank_size, total_cols)
    weights = block_diagonals(translations[0])
    low_bits = lax.axis_size("gy").bit_length() - 1
    high_bits = lax.axis_size("gx").bit_length() - 1
    levels = [("gy", bit) for bit in range(low_bits)] + [("gx", bit) for bit in range(high_bits)]
    last = len(levels) - 1
    take_at, own_at, first_at, second_at, own_late_at = (min(k, last) for k in (1, 2, 4, 5, 6))
    padded = extended(ordered, ((("gx", "gy"), 1),), HW * leaf_size)
    blocks_all = padded.reshape(rhs_count, leaf_count + 2 * HW, leaf_size)
    block_index = jnp.arange(leaf_count, dtype=jnp.int32) + HW + band_offsets
    half = leaf_count // 2
    coeffs = coeffs.reshape(rank_size, group_total, group_width).transpose(1, 0, 2)
    coeffs = coeffs.reshape(group_total * rank_size, group_width)
    picked = None
    for level, (axis, bit) in enumerate(levels):
        if level == take_at:
            coeffs, blocks_all = lax.optimization_barrier((coeffs, blocks_all))
            picked = jnp.take(blocks_all, block_index, axis=1)
        if level == own_at:
            coeffs, own_first = lax.optimization_barrier((coeffs, leaves[:, :half]))
        if level == own_late_at:
            coeffs, own_second = lax.optimization_barrier((coeffs, leaves[:, half:]))
        if level == first_at:
            coeffs, picked_first = lax.optimization_barrier((coeffs, picked[:, :half]))
        if level == second_at:
            coeffs, picked_second = lax.optimization_barrier((coeffs, picked[:, half:]))
        partner = from_partner(coeffs, axis, bit)
        coeffs = translate(weights[level], coeffs, partner)
    coeffs = coeffs.reshape(group_total, rank_size, group_width).transpose(1, 0, 2)
    coeffs = coeffs.reshape(rank_size, total_cols)
    coeff_bf = coeffs.astype(jnp.bfloat16).reshape(rank_size, leaf_count, rhs_count)
    far_term = jnp.einsum("lrp,rls->slp", out_basis, coeff_bf, preferred_element_type=jnp.float32)
    own_term = jnp.concatenate(
        [
            jnp.einsum("lpq,slq->slp", band_blocks[:half, 0], own_first, preferred_element_type=jnp.float32),
            jnp.einsum("lpq,slq->slp", band_blocks[half:, 0], own_second, preferred_element_type=jnp.float32),
        ],
        axis=1,
    )
    partner_first = jnp.einsum(
        "lpq,slq->slp", band_blocks[:half, 1], picked_first, preferred_element_type=jnp.float32
    )
    partner_second = jnp.einsum(
        "lpq,slq->slp", band_blocks[half:, 1], picked_second, preferred_element_type=jnp.float32
    )
    partner_term = jnp.concatenate([partner_first, partner_second], axis=1)
    return (far_term + own_term + partner_term).reshape(rhs_count, point_count)


def solution(mesh):
    return jax.shard_map(
        local,
        mesh=mesh,
        in_specs=(
            P(None, ("gx", "gy")),
            P(("gx", "gy")),
            P(("gx", "gy")),
            P(("gx", "gy"), None, None),
            P(("gx", "gy"), None, None, None),
            P(("gx", "gy"), None, None, None, None, None),
            P(("gx", "gy"), None, None),
        ),
        out_specs=P(None, ("gx", "gy")),
        check_vma=False,
    )
```

```python
import jax
import jax.numpy as jnp
from jax import lax
from jax.experimental import pallas as pl
from jax.experimental.pallas import tpu as pltpu
from jax.sharding import PartitionSpec as P

HW = 16


CHUNK = 128
PARTS = 4


def gather_kernel(idx_ref, x_hbm, o_ref, x_ref, xt_ref, sems):
    count = o_ref.shape[1]
    span = count // PARTS
    fetches = [
        pltpu.make_async_copy(x_hbm.at[:, pl.ds(q * span, span)], x_ref.at[:, pl.ds(q * span, span)], sems.at[q])
        for q in range(PARTS)
    ]
    for fetch in fetches:
        fetch.start()
    for q, fetch in enumerate(fetches):
        fetch.wait()

        def spread(c, carry, q=q):
            col = pl.multiple_of(q * span + c * CHUNK, CHUNK)
            xt_ref[pl.ds(col, CHUNK), :] = x_ref[:, pl.ds(col, CHUNK)].T
            return carry

        lax.fori_loop(0, span // CHUNK, spread, 0, unroll=4)

    def body(c, carry):
        col = pl.multiple_of(c * CHUNK, CHUNK)
        rows = [xt_ref[pl.ds(idx_ref[col + u], 1), :] for u in range(CHUNK)]
        o_ref[:, pl.ds(col, CHUNK)] = jnp.concatenate(rows, axis=0).T.astype(o_ref.dtype)
        return carry

    lax.fori_loop(0, count // CHUNK, body, 0, unroll=16)


def gather_points(points, index):
    width, count = points.shape
    return pl.pallas_call(
        gather_kernel,
        out_shape=jax.ShapeDtypeStruct((width, count), jnp.bfloat16),
        in_specs=[pl.BlockSpec(memory_space=pltpu.SMEM), pl.BlockSpec(memory_space=pl.ANY)],
        out_specs=pl.BlockSpec(memory_space=pltpu.VMEM),
        scratch_shapes=[
            pltpu.VMEM((width, count), jnp.float32),
            pltpu.VMEM((count, width), jnp.float32),
            pltpu.SemaphoreType.DMA((PARTS,)),
        ],
        compiler_params=pltpu.CompilerParams(vmem_limit_bytes=67043328),
        cost_estimate=pl.CostEstimate(flops=0, transcendentals=0, bytes_accessed=count * width * 6),
    )(index, points)


def from_partner(x, axis, distance):
    return lax.ppermute(x, axis, [(i, i ^ 1 << distance) for i in range(lax.axis_size(axis))])


def extended(x, sides, width):
    for axis, dim in sides:
        count, length = (lax.axis_size(axis), x.shape[dim])
        up = [(i, (i + 1) % count) for i in range(count - 1)]
        down = [(j, i) for i, j in up]
        last = lax.slice_in_dim(x, length - width, length, axis=dim)
        initial = lax.slice_in_dim(x, 0, width, axis=dim)
        before = lax.ppermute(last, axis, up)
        after = lax.ppermute(initial, axis, down)
        x = jnp.concatenate([before, x, after], axis=dim)
    return x


def block_diagonals(weights):
    levels, groups, terms, rank, _ = weights.shape
    width = groups * rank
    shape = (groups, rank, width)
    target = lax.broadcasted_iota(jnp.int32, shape, 0) * rank + lax.broadcasted_iota(jnp.int32, shape, 1)
    spread = (lax.broadcasted_iota(jnp.int32, shape, 2) == target).astype(weights.dtype)
    return jnp.einsum(
        "lgtab,gbc->ltgac", weights, spread, precision=lax.Precision.HIGHEST, preferred_element_type=jnp.float32
    ).reshape(levels, terms, width, width)


def translate(level_matrices, own_coeffs, other_coeffs):
    first = jnp.dot(
        level_matrices[0],
        own_coeffs,
        precision=lax.Precision.HIGH,
        preferred_element_type=jnp.float32,
    )
    second = jnp.dot(
        level_matrices[1],
        other_coeffs,
        precision=lax.Precision.HIGH,
        preferred_element_type=jnp.float32,
    )
    return first + second


def local(points_rhs, morton_order, band_offsets, leaf_basis, band_blocks, translations, out_basis):
    rhs_count, point_count = points_rhs.shape
    leaf_count, rank_size, leaf_size = leaf_basis.shape
    group_total = translations.shape[2]
    total_cols = leaf_count * rhs_count
    group_width = total_cols // group_total
    ordered = gather_points(points_rhs, morton_order)
    leaves = ordered.reshape(rhs_count, leaf_count, leaf_size)
    coeffs = jnp.einsum(
        "lrp,slp->rls", leaf_basis, leaves, preferred_element_type=jnp.float32
    ).reshape(rank_size, total_cols)
    weights = block_diagonals(translations[0])
    low_bits = lax.axis_size("gy").bit_length() - 1
    high_bits = lax.axis_size("gx").bit_length() - 1
    levels = [("gy", bit) for bit in range(low_bits)] + [("gx", bit) for bit in range(high_bits)]
    last = len(levels) - 1
    take_at, own_at, first_at, second_at, own_late_at = (min(k, last) for k in (1, 2, 4, 5, 6))
    padded = extended(ordered, ((("gx", "gy"), 1),), HW * leaf_size)
    blocks_all = padded.reshape(rhs_count, leaf_count + 2 * HW, leaf_size)
    block_index = jnp.arange(leaf_count, dtype=jnp.int32) + HW + band_offsets
    half = leaf_count // 2
    coeffs = coeffs.reshape(rank_size, group_total, group_width).transpose(1, 0, 2)
    coeffs = coeffs.reshape(group_total * rank_size, group_width)
    picked = None
    for level, (axis, bit) in enumerate(levels):
        if level == take_at:
            coeffs, blocks_all = lax.optimization_barrier((coeffs, blocks_all))
            picked = jnp.take(blocks_all, block_index, axis=1)
        if level == own_at:
            coeffs, own_first = lax.optimization_barrier((coeffs, leaves[:, :half]))
        if level == own_late_at:
            coeffs, own_second = lax.optimization_barrier((coeffs, leaves[:, half:]))
        if level == first_at:
            coeffs, picked_first = lax.optimization_barrier((coeffs, picked[:, :half]))
        if level == second_at:
            coeffs, picked_second = lax.optimization_barrier((coeffs, picked[:, half:]))
        partner = from_partner(coeffs, axis, bit)
        coeffs = translate(weights[level], coeffs, partner)
    coeffs = coeffs.reshape(group_total, rank_size, group_width).transpose(1, 0, 2)
    coeffs = coeffs.reshape(rank_size, total_cols)
    coeff_bf = coeffs.astype(jnp.bfloat16).reshape(rank_size, leaf_count, rhs_count)
    far_term = jnp.einsum("lrp,rls->slp", out_basis, coeff_bf, preferred_element_type=jnp.float32)
    own_term = jnp.concatenate(
        [
            jnp.einsum("lpq,slq->slp", band_blocks[:half, 0], own_first, preferred_element_type=jnp.float32),
            jnp.einsum("lpq,slq->slp", band_blocks[half:, 0], own_second, preferred_element_type=jnp.float32),
        ],
        axis=1,
    )
    partner_first = jnp.einsum(
        "lpq,slq->slp", band_blocks[:half, 1], picked_first, preferred_element_type=jnp.float32
    )
    partner_second = jnp.einsum(
        "lpq,slq->slp", band_blocks[half:, 1], picked_second, preferred_element_type=jnp.float32
    )
    partner_term = jnp.concatenate([partner_first, partner_second], axis=1)
    return (far_term + own_term + partner_term).reshape(rhs_count, point_count)


def solution(mesh):
    return jax.shard_map(
        local,
        mesh=mesh,
        in_specs=(
            P(None, ("gx", "gy")),
            P(("gx", "gy")),
            P(("gx", "gy")),
            P(("gx", "gy"), None, None),
            P(("gx", "gy"), None, None, None),
            P(("gx", "gy"), None, None, None, None, None),
            P(("gx", "gy"), None, None),
        ),
        out_specs=P(None, ("gx", "gy")),
        check_vma=False,
    )
```

```python
import jax
import jax.numpy as jnp
from jax import lax
from jax.experimental import pallas as pl
from jax.experimental.pallas import tpu as pltpu
from jax.sharding import PartitionSpec as P

HW = 16


CHUNK = 128
PARTS = 4


def gather_kernel(idx_ref, x_hbm, o_ref, x_ref, xt_ref, sems):
    count = o_ref.shape[1]
    span = count // PARTS
    fetches = [
        pltpu.make_async_copy(x_hbm.at[:, pl.ds(q * span, span)], x_ref.at[:, pl.ds(q * span, span)], sems.at[q])
        for q in range(PARTS)
    ]
    for fetch in fetches:
        fetch.start()
    for q, fetch in enumerate(fetches):
        fetch.wait()

        def spread(c, carry, q=q):
            col = pl.multiple_of(q * span + c * CHUNK, CHUNK)
            xt_ref[pl.ds(col, CHUNK), :] = x_ref[:, pl.ds(col, CHUNK)].T
            return carry

        lax.fori_loop(0, span // CHUNK, spread, 0, unroll=4)

    def body(c, carry):
        col = pl.multiple_of(c * CHUNK, CHUNK)
        rows = [xt_ref[pl.ds(idx_ref[col + u], 1), :] for u in range(CHUNK)]
        o_ref[:, pl.ds(col, CHUNK)] = jnp.concatenate(rows, axis=0).T.astype(o_ref.dtype)
        return carry

    lax.fori_loop(0, count // CHUNK, body, 0, unroll=32)


def gather_points(points, index):
    width, count = points.shape
    return pl.pallas_call(
        gather_kernel,
        out_shape=jax.ShapeDtypeStruct((width, count), jnp.bfloat16),
        in_specs=[pl.BlockSpec(memory_space=pltpu.SMEM), pl.BlockSpec(memory_space=pl.ANY)],
        out_specs=pl.BlockSpec(memory_space=pltpu.VMEM),
        scratch_shapes=[
            pltpu.VMEM((width, count), jnp.float32),
            pltpu.VMEM((count, width), jnp.float32),
            pltpu.SemaphoreType.DMA((PARTS,)),
        ],
        compiler_params=pltpu.CompilerParams(vmem_limit_bytes=67043328),
        cost_estimate=pl.CostEstimate(flops=0, transcendentals=0, bytes_accessed=count * width * 6),
    )(index, points)


def from_partner(x, axis, distance):
    return lax.ppermute(x, axis, [(i, i ^ 1 << distance) for i in range(lax.axis_size(axis))])


def extended(x, sides, width):
    for axis, dim in sides:
        count, length = (lax.axis_size(axis), x.shape[dim])
        up = [(i, (i + 1) % count) for i in range(count - 1)]
        down = [(j, i) for i, j in up]
        last = lax.slice_in_dim(x, length - width, length, axis=dim)
        initial = lax.slice_in_dim(x, 0, width, axis=dim)
        before = lax.ppermute(last, axis, up)
        after = lax.ppermute(initial, axis, down)
        x = jnp.concatenate([before, x, after], axis=dim)
    return x


def block_diagonals(weights):
    levels, groups, terms, rank, _ = weights.shape
    width = groups * rank
    shape = (groups, rank, width)
    target = lax.broadcasted_iota(jnp.int32, shape, 0) * rank + lax.broadcasted_iota(jnp.int32, shape, 1)
    spread = (lax.broadcasted_iota(jnp.int32, shape, 2) == target).astype(weights.dtype)
    return jnp.einsum(
        "lgtab,gbc->ltgac", weights, spread, precision=lax.Precision.HIGHEST, preferred_element_type=jnp.float32
    ).reshape(levels, terms, width, width)


def translate(level_matrices, own_coeffs, other_coeffs):
    first = jnp.dot(
        level_matrices[0],
        own_coeffs,
        precision=lax.Precision.HIGH,
        preferred_element_type=jnp.float32,
    )
    second = jnp.dot(
        level_matrices[1],
        other_coeffs,
        precision=lax.Precision.HIGH,
        preferred_element_type=jnp.float32,
    )
    return first + second


def local(points_rhs, morton_order, band_offsets, leaf_basis, band_blocks, translations, out_basis):
    rhs_count, point_count = points_rhs.shape
    leaf_count, rank_size, leaf_size = leaf_basis.shape
    group_total = translations.shape[2]
    total_cols = leaf_count * rhs_count
    group_width = total_cols // group_total
    ordered = gather_points(points_rhs, morton_order)
    leaves = ordered.reshape(rhs_count, leaf_count, leaf_size)
    coeffs = jnp.einsum(
        "lrp,slp->rls", leaf_basis, leaves, preferred_element_type=jnp.float32
    ).reshape(rank_size, total_cols)
    weights = block_diagonals(translations[0])
    low_bits = lax.axis_size("gy").bit_length() - 1
    high_bits = lax.axis_size("gx").bit_length() - 1
    levels = [("gy", bit) for bit in range(low_bits)] + [("gx", bit) for bit in range(high_bits)]
    last = len(levels) - 1
    take_at, own_at, first_at, second_at, own_late_at = (min(k, last) for k in (1, 2, 4, 5, 6))
    padded = extended(ordered, ((("gx", "gy"), 1),), HW * leaf_size)
    blocks_all = padded.reshape(rhs_count, leaf_count + 2 * HW, leaf_size)
    block_index = jnp.arange(leaf_count, dtype=jnp.int32) + HW + band_offsets
    half = leaf_count // 2
    coeffs = coeffs.reshape(rank_size, group_total, group_width).transpose(1, 0, 2)
    coeffs = coeffs.reshape(group_total * rank_size, group_width)
    picked = None
    for level, (axis, bit) in enumerate(levels):
        if level == take_at:
            coeffs, blocks_all = lax.optimization_barrier((coeffs, blocks_all))
            picked = jnp.take(blocks_all, block_index, axis=1)
        if level == own_at:
            coeffs, own_first = lax.optimization_barrier((coeffs, leaves[:, :half]))
        if level == own_late_at:
            coeffs, own_second = lax.optimization_barrier((coeffs, leaves[:, half:]))
        if level == first_at:
            coeffs, picked_first = lax.optimization_barrier((coeffs, picked[:, :half]))
        if level == second_at:
            coeffs, picked_second = lax.optimization_barrier((coeffs, picked[:, half:]))
        partner = from_partner(coeffs, axis, bit)
        coeffs = translate(weights[level], coeffs, partner)
    coeffs = coeffs.reshape(group_total, rank_size, group_width).transpose(1, 0, 2)
    coeffs = coeffs.reshape(rank_size, total_cols)
    coeff_bf = coeffs.astype(jnp.bfloat16).reshape(rank_size, leaf_count, rhs_count)
    far_term = jnp.einsum("lrp,rls->slp", out_basis, coeff_bf, preferred_element_type=jnp.float32)
    own_term = jnp.concatenate(
        [
            jnp.einsum("lpq,slq->slp", band_blocks[:half, 0], own_first, preferred_element_type=jnp.float32),
            jnp.einsum("lpq,slq->slp", band_blocks[half:, 0], own_second, preferred_element_type=jnp.float32),
        ],
        axis=1,
    )
    partner_first = jnp.einsum(
        "lpq,slq->slp", band_blocks[:half, 1], picked_first, preferred_element_type=jnp.float32
    )
    partner_second = jnp.einsum(
        "lpq,slq->slp", band_blocks[half:, 1], picked_second, preferred_element_type=jnp.float32
    )
    partner_term = jnp.concatenate([partner_first, partner_second], axis=1)
    return (far_term + own_term + partner_term).reshape(rhs_count, point_count)


def solution(mesh):
    return jax.shard_map(
        local,
        mesh=mesh,
        in_specs=(
            P(None, ("gx", "gy")),
            P(("gx", "gy")),
            P(("gx", "gy")),
            P(("gx", "gy"), None, None),
            P(("gx", "gy"), None, None, None),
            P(("gx", "gy"), None, None, None, None, None),
            P(("gx", "gy"), None, None),
        ),
        out_specs=P(None, ("gx", "gy")),
        check_vma=False,
    )
```
